128 devices in a mesh: blk: 8 (over y_lo, x), dom: 16 (over y_hi, z, core).
Axes of the slice: x: 4, y: 4 (y_hi: 2, y_lo: 2; y = y_hi * 2 + y_lo), z: 4, core: 2. Of those that a mesh axis runs over, the one named last changes fastest.
Arguments:
- source_emb: bfloat16 [16384, 64], P(('blk', 'dom')), may hold values from -6 to 6
- target_emb: bfloat16 [98304, 64], P(('blk', 'dom')), may hold values from -6 to 6
- source_counts: int32 [16384, 128], P(('blk', 'dom')), may hold values from 1 to 4
- target_counts: int32 [98304, 128], P(('blk', 'dom')), may hold values from 1 to 4
- warm_start: float32 [98304, 128], P(('blk', 'dom')), may hold values from -8 to 263
Outputs:
- source_log_scaling: float32 [16384, 128], P(('blk', 'dom'))
- target_log_scaling: float32 [98304, 128], P(('blk', 'dom'))
The draws below stay inside these ranges and needn't reach their ends.
All inputs are finite; a program needn't handle non-finite values.
Results may differ from the reference program's by a relative error of at most 0.0022.
Values may be sent and summed in bfloat16 or wider, within the bound.
No kernel may reach another device: no remote copies, remote signals or barrier semaphores. Data moves between devices by JAX's collectives and lax.ppermute only.
A program may use at most 64 MiB of HBM per device.

```python
import math
import jax
import jax.numpy as jnp
from jax import lax

D = 64
B = 128
ITERS = 2
NS = 16384
NT = 98304


def draw_warm_start(key, part):
    first_key = jax.random.fold_in(key, 0)
    return jnp.clip(2.0 * jax.random.normal(first_key, (NT, B), jnp.float32), -8.0, 8.0)


def place_ends(values, own_key, smallest, largest):
    shape = values.shape
    index_at = [jax.random.randint(jax.random.fold_in(own_key, axis), (), 0, shape[axis]) for axis in range(len(shape))]
    values = values.at[tuple(index_at)].set(smallest)
    longest = shape.index(max(shape))
    index_at[longest] = (index_at[longest] + 1) % shape[longest]
    return values.at[tuple(index_at)].set(largest)


def steps_of(stream_key, extent, cuts, least, high):
    def one(position, shards_of):
        heights = jax.random.uniform(jax.random.fold_in(jax.random.fold_in(stream_key, 6), position), (shards_of,), jnp.float32, least / len(cuts), high / len(cuts))
        return jnp.repeat(jnp.exp(heights), extent[position] // shards_of).reshape((-1,) + (1,) * (len(extent) - position - 1))

    gain = one(*cuts[0])
    for cut in cuts[1:]:
        gain = gain * one(*cut)
    return gain


def centred(rng, dims, scale, reach, pieces=(), dtype=jnp.bfloat16):
    gain = steps_of(rng, dims, pieces, -0.22, 0.18) if pieces else 1.0
    array = jax.random.normal(rng, dims, jnp.float32) * scale * gain
    return jnp.minimum(jnp.maximum(array, -reach), reach).astype(dtype)


def setup_inputs(seed: int = 0) -> dict:
    splits = jax.random.split(jax.random.key(seed), 6)
    source_emb = centred(splits[0], (NS, D), 1.0, 6.0, ((0, 128),))
    target_emb = centred(splits[1], (NT, D), 1.0, 6.0, ((0, 128),))
    source_counts = place_ends(jax.random.randint(splits[2], (NS, B), 1, 5), jax.random.fold_in(splits[2], 1), 1, 4).astype(jnp.int32)
    target_counts = place_ends(jax.random.randint(splits[3], (NT, B), 1, 5), jax.random.fold_in(splits[3], 1), 1, 4).astype(jnp.int32)
    warm_start = draw_warm_start(jax.random.fold_in(splits[5], 71), 0)
    return {"source_emb": source_emb, "target_emb": target_emb, "source_counts": source_counts, "target_counts": target_counts, "warm_start": warm_start}


entropic = 0.05

def normalized(values):
    widened = values.astype(jnp.float32)
    squared = lax.optimization_barrier(jnp.sum(widened * widened, axis=1, keepdims=True)) + 1e-06
    return (widened * lax.rsqrt(squared)).astype(jnp.bfloat16)

def kernel_sums(row_emb, col_emb, col_weights):
    row_count = row_emb.shape[0]
    col_count = col_emb.shape[0]
    row_block = math.gcd(row_count, 512)
    col_block = math.gcd(col_count, 2048)
    row_parts = row_emb.reshape(row_count // row_block, row_block, row_emb.shape[1])
    col_parts = col_emb.reshape(col_count // col_block, col_block, col_emb.shape[1])
    weight_parts = col_weights.reshape(col_count // col_block, col_block, col_weights.shape[1])

    def one_block(row_piece):

        def add_block(running, paired):
            col_piece, weight_piece = paired
            products = jnp.dot(row_piece, col_piece.T, preferred_element_type=jnp.float32)
            kernel = jnp.exp((products - 1.0) / entropic).astype(jnp.bfloat16)
            return (running + jnp.dot(kernel, weight_piece, preferred_element_type=jnp.float32), None)
        initial = jnp.zeros((row_piece.shape[0], col_weights.shape[1]), jnp.float32)
        result, unused = lax.scan(add_block, initial, (col_parts, weight_parts))
        return result
    return lax.map(one_block, row_parts).reshape(row_count, col_weights.shape[1])

def reference(source_emb, target_emb, source_counts, target_counts, warm_start):
    source_unit = normalized(source_emb)
    target_unit = normalized(target_emb)
    log_source = jnp.log(source_counts.astype(jnp.float32)) - math.log(NS)
    log_target = jnp.log(target_counts.astype(jnp.float32)) - math.log(NT)
    target_logs = warm_start
    source_logs = jnp.zeros((NS, B), jnp.float32)
    for iteration in range(ITERS):
        target_peak = lax.optimization_barrier(jnp.max(target_logs, axis=0))
        target_weights = jnp.exp(target_logs - target_peak).astype(jnp.bfloat16)
        source_sums = kernel_sums(source_unit, target_unit, target_weights)
        source_logs = log_source - target_peak - jnp.log(source_sums)
        source_peak = lax.optimization_barrier(jnp.max(source_logs, axis=0))
        source_weights = jnp.exp(source_logs - source_peak).astype(jnp.bfloat16)
        target_sums = kernel_sums(target_unit, source_unit, source_weights)
        target_logs = log_target - source_peak - jnp.log(target_sums)
    return (source_logs, target_logs)
```

```python
import math

import jax
import jax.numpy as jnp
from jax import lax
from jax.sharding import PartitionSpec as P

ITERS = 2


entropic = 0.05


def normalized(values):
    widened = values.astype(jnp.float32)
    squared = jnp.sum(widened * widened, axis=1, keepdims=True) + 1e-06
    return (widened * lax.rsqrt(squared)).astype(jnp.bfloat16)


def kernel_block(row_piece, col_piece):
    products = jnp.dot(row_piece, col_piece.T, preferred_element_type=jnp.float32)
    return jnp.exp((products - 1.0) / entropic).astype(jnp.bfloat16)


def segment_sums(row_emb, col_segments, weight_segments, factors, row_block):
    row_count = row_emb.shape[0]
    row_parts = row_emb.reshape(row_count // row_block, row_block, row_emb.shape[1])

    def one_block(row_piece):

        def add_segment(running, paired):
            col_piece, weight_piece, factor = paired
            kernel = kernel_block(row_piece, col_piece)
            part = jnp.dot(kernel, weight_piece, preferred_element_type=jnp.float32)
            return (running + factor[None, :] * part, None)

        initial = jnp.zeros((row_piece.shape[0], weight_segments.shape[-1]), jnp.float32)
        result, unused = lax.scan(add_segment, initial, (col_segments, weight_segments, factors))
        return result

    return lax.map(one_block, row_parts).reshape(row_count, weight_segments.shape[-1])


def plain_sums(row_emb, col_emb, col_weights, row_block, col_block):
    col_count = col_emb.shape[0]
    segments = col_count // col_block
    return segment_sums(
        row_emb,
        col_emb.reshape(segments, col_block, col_emb.shape[1]),
        col_weights.reshape(segments, col_block, col_weights.shape[1]),
        jnp.ones((segments, col_weights.shape[1]), jnp.float32),
        row_block,
    )


def permute_gather(value, axis, count):
    me = lax.axis_index(axis)
    received = [value]
    for shift in range(1, count):
        received.append(lax.ppermute(value, axis, [(i, (i + shift) % count) for i in range(count)]))
    stacked = jnp.stack(received[::-1], 0)
    return jnp.roll(stacked, me + 1, axis=0)


def shift_of(values):
    return jnp.max(values, axis=0).astype(jnp.bfloat16).astype(jnp.float32)


def padded_rows(rows, multiple):
    return -(-rows // multiple) * multiple


def body(source_emb, target_emb, source_counts, target_counts, warm_start):
    blk_count = lax.axis_size("blk")
    dom_count = lax.axis_size("dom")
    src_rows = source_emb.shape[0]
    tgt_rows = target_emb.shape[0]
    columns = warm_start.shape[1]
    width = source_emb.shape[1]
    all_sources = src_rows * blk_count * dom_count
    all_targets = tgt_rows * blk_count * dom_count
    block_rows = src_rows * dom_count
    group_rows = tgt_rows * blk_count

    source_block = lax.all_gather(normalized(source_emb), "dom", axis=0, tiled=True)
    own_targets = normalized(target_emb)
    log_target = jnp.log(target_counts.astype(jnp.float32)) - math.log(all_targets)
    log_source = jnp.log(source_counts.astype(jnp.float32)) - math.log(all_sources)

    tgt_payload_rows = padded_rows(tgt_rows + 1, 16)
    src_piece_rows = padded_rows(src_rows + 1, 8)
    tgt_piece_rows = padded_rows(tgt_rows + 1, 8)

    target_logs = warm_start
    target_group = None
    source_logs = None
    for iteration in range(ITERS):
        shift = shift_of(target_logs)
        weights = jnp.exp(target_logs - shift).astype(jnp.bfloat16)
        payload = jnp.concatenate(
            [weights, shift.astype(jnp.bfloat16)[None, :],
             jnp.zeros((tgt_payload_rows - tgt_rows - 1, columns), jnp.bfloat16)], axis=0)
        if target_group is None:
            emb_rows = jnp.concatenate(
                [own_targets, jnp.zeros((tgt_payload_rows - tgt_rows, width), jnp.bfloat16)], axis=0)
            payload = jnp.concatenate([emb_rows, payload], axis=1)
            gathered = permute_gather(payload, "blk", blk_count)
            target_group = gathered[:, :tgt_rows, :width].reshape(group_rows, width)
            gathered = gathered[:, :, width:]
        else:
            gathered = permute_gather(payload, "blk", blk_count)
        weight_segments = gathered[:, :tgt_rows, :]
        segment_shift = gathered[:, tgt_rows, :].astype(jnp.float32)
        group_shift = jnp.max(segment_shift, axis=0)
        factors = jnp.exp(segment_shift - group_shift[None, :])
        partial_value = segment_sums(
            source_block,
            target_group.reshape(blk_count, tgt_rows, width),
            weight_segments,
            factors,
            min(block_rows, 1024),
        )
        pieces = jnp.concatenate(
            [partial_value.reshape(dom_count, src_rows, columns),
             jnp.broadcast_to(group_shift[None, None, :], (dom_count, 1, columns)),
             jnp.zeros((dom_count, src_piece_rows - src_rows - 1, columns), jnp.float32)], axis=1)
        received = lax.all_to_all(pieces, "dom", 0, 0, tiled=False)
        group_shifts = received[:, src_rows, :]
        target_peak = jnp.max(group_shifts, axis=0)
        scale = jnp.exp(group_shifts - target_peak[None, :])
        shares = jnp.sum(received[:, :src_rows, :] * scale[:, None, :], axis=0)
        source_logs = log_source - target_peak - jnp.log(shares)

        block_logs = lax.all_gather(source_logs, "dom", axis=0, tiled=True)
        block_peak = jnp.max(block_logs, axis=0)
        source_weights = jnp.exp(block_logs - block_peak).astype(jnp.bfloat16)
        target_partial = plain_sums(target_group, source_block, source_weights, 1024, block_rows)
        pieces = jnp.concatenate(
            [target_partial.reshape(blk_count, tgt_rows, columns),
             jnp.broadcast_to(block_peak[None, None, :], (blk_count, 1, columns)),
             jnp.zeros((blk_count, tgt_piece_rows - tgt_rows - 1, columns), jnp.float32)], axis=1)
        received = lax.all_to_all(pieces, "blk", 0, 0, tiled=False)
        block_peaks = received[:, tgt_rows, :]
        source_peak = jnp.max(block_peaks, axis=0)
        scale = jnp.exp(block_peaks - source_peak[None, :])
        target_sums = jnp.sum(received[:, :tgt_rows, :] * scale[:, None, :], axis=0)
        target_logs = log_target - source_peak - jnp.log(target_sums)
    return (source_logs, target_logs)


def solution(mesh):
    in_specs = (
        P(("blk", "dom"), None),
        P(("blk", "dom"), None),
        P(("blk", "dom"), None),
        P(("blk", "dom"), None),
        P(("blk", "dom"), None),
    )
    out_specs = (P(("blk", "dom"), None), P(("blk", "dom"), None))
    return jax.shard_map(body, mesh=mesh, in_specs=in_specs, out_specs=out_specs, check_vma=False)
```

```python
import math

import jax
import jax.numpy as jnp
from jax import lax
from jax.sharding import PartitionSpec as P

ITERS = 2


entropic = 0.05


def normalized(values):
    widened = values.astype(jnp.float32)
    squared = jnp.sum(widened * widened, axis=1, keepdims=True) + 1e-06
    return (widened * lax.rsqrt(squared)).astype(jnp.bfloat16)


def kernel_block(row_piece, col_piece):
    products = jnp.dot(row_piece, col_piece.T, preferred_element_type=jnp.float32)
    return jnp.exp((products - 1.0) / entropic).astype(jnp.bfloat16)


def segment_sums(row_emb, col_segments, weight_segments, factors, row_block):
    row_count = row_emb.shape[0]
    row_parts = row_emb.reshape(row_count // row_block, row_block, row_emb.shape[1])

    def one_block(row_piece):

        def add_segment(running, paired):
            col_piece, weight_piece, factor = paired
            kernel = kernel_block(row_piece, col_piece)
            part = jnp.dot(kernel, weight_piece, preferred_element_type=jnp.float32)
            return (running + factor[None, :] * part, None)

        initial = jnp.zeros((row_piece.shape[0], weight_segments.shape[-1]), jnp.float32)
        result, unused = lax.scan(add_segment, initial, (col_segments, weight_segments, factors))
        return result

    return lax.map(one_block, row_parts).reshape(row_count, weight_segments.shape[-1])


def plain_sums(row_emb, col_emb, col_weights, row_block, col_block):
    col_count = col_emb.shape[0]
    segments = col_count // col_block
    return segment_sums(
        row_emb,
        col_emb.reshape(segments, col_block, col_emb.shape[1]),
        col_weights.reshape(segments, col_block, col_weights.shape[1]),
        jnp.ones((segments, col_weights.shape[1]), jnp.float32),
        row_block,
    )


def permute_gather(value, axis, count):
    me = lax.axis_index(axis)
    received = [value]
    for shift in range(1, count):
        received.append(lax.ppermute(value, axis, [(i, (i + shift) % count) for i in range(count)]))
    stacked = jnp.stack(received[::-1], 0)
    return jnp.roll(stacked, me + 1, axis=0)


def shift_of(values):
    return jnp.max(values, axis=0).astype(jnp.bfloat16).astype(jnp.float32)


def padded_rows(rows, multiple):
    return -(-rows // multiple) * multiple


def body(source_emb, target_emb, source_counts, target_counts, warm_start):
    blk_count = lax.axis_size("blk")
    dom_count = lax.axis_size("dom")
    src_rows = source_emb.shape[0]
    tgt_rows = target_emb.shape[0]
    columns = warm_start.shape[1]
    width = source_emb.shape[1]
    all_sources = src_rows * blk_count * dom_count
    all_targets = tgt_rows * blk_count * dom_count
    block_rows = src_rows * dom_count
    group_rows = tgt_rows * blk_count

    source_block = lax.all_gather(normalized(source_emb), "dom", axis=0, tiled=True)
    own_targets = normalized(target_emb)
    log_target = jnp.log(target_counts.astype(jnp.float32)) - math.log(all_targets)
    log_source = jnp.log(source_counts.astype(jnp.float32)) - math.log(all_sources)

    tgt_payload_rows = padded_rows(tgt_rows + 1, 16)
    src_piece_rows = padded_rows(src_rows + 1, 8)
    tgt_piece_rows = padded_rows(tgt_rows + 1, 8)

    target_logs = warm_start
    target_group = None
    source_logs = None
    kernel = None
    for iteration in range(ITERS):
        shift = shift_of(target_logs)
        weights = jnp.exp(target_logs - shift).astype(jnp.bfloat16)
        payload = jnp.concatenate(
            [weights, shift.astype(jnp.bfloat16)[None, :],
             jnp.zeros((tgt_payload_rows - tgt_rows - 1, columns), jnp.bfloat16)], axis=0)
        if target_group is None:
            emb_rows = jnp.concatenate(
                [own_targets, jnp.zeros((tgt_payload_rows - tgt_rows, width), jnp.bfloat16)], axis=0)
            payload = jnp.concatenate([emb_rows, payload], axis=1)
            gathered = permute_gather(payload, "blk", blk_count)
            target_group = gathered[:, :tgt_rows, :width].reshape(group_rows, width)
            gathered = gathered[:, :, width:]
        else:
            gathered = permute_gather(payload, "blk", blk_count)
        weight_segments = gathered[:, :tgt_rows, :]
        segment_shift = gathered[:, tgt_rows, :].astype(jnp.float32)
        group_shift = jnp.max(segment_shift, axis=0)
        factors = jnp.exp(segment_shift - group_shift[None, :])
        if kernel is None:
            products = jnp.einsum(
                "id,sjd->sij", source_block, target_group.reshape(blk_count, tgt_rows, width),
                preferred_element_type=jnp.float32)
            kernel = jnp.exp((products - 1.0) / entropic).astype(jnp.bfloat16)
        per_segment = jnp.einsum(
            "sij,sjc->sic", kernel, weight_segments, preferred_element_type=jnp.float32)
        partial_value = jnp.sum(per_segment * factors[:, None, :], axis=0)
        pieces = jnp.concatenate(
            [partial_value.reshape(dom_count, src_rows, columns),
             jnp.broadcast_to(group_shift[None, None, :], (dom_count, 1, columns)),
             jnp.zeros((dom_count, src_piece_rows - src_rows - 1, columns), jnp.float32)], axis=1)
        received = lax.all_to_all(pieces, "dom", 0, 0, tiled=False)
        group_shifts = received[:, src_rows, :]
        target_peak = jnp.max(group_shifts, axis=0)
        scale = jnp.exp(group_shifts - target_peak[None, :])
        shares = jnp.sum(received[:, :src_rows, :] * scale[:, None, :], axis=0)
        source_logs = log_source - target_peak - jnp.log(shares)

        block_logs = lax.all_to_all(
            jnp.broadcast_to(source_logs[None], (dom_count, src_rows, columns)), "dom", 0, 0, tiled=False
        ).reshape(block_rows, columns)
        block_peak = jnp.max(block_logs, axis=0)
        source_weights = jnp.exp(block_logs - block_peak).astype(jnp.bfloat16)
        target_partial = jnp.einsum(
            "ic,sij->sjc", source_weights, kernel, preferred_element_type=jnp.float32
        ).reshape(group_rows, columns)
        pieces = jnp.concatenate(
            [target_partial.reshape(blk_count, tgt_rows, columns),
             jnp.broadcast_to(block_peak[None, None, :], (blk_count, 1, columns)),
             jnp.zeros((blk_count, tgt_piece_rows - tgt_rows - 1, columns), jnp.float32)], axis=1)
        received = lax.all_to_all(pieces, "blk", 0, 0, tiled=False)
        block_peaks = received[:, tgt_rows, :]
        source_peak = jnp.max(block_peaks, axis=0)
        scale = jnp.exp(block_peaks - source_peak[None, :])
        target_sums = jnp.sum(received[:, :tgt_rows, :] * scale[:, None, :], axis=0)
        target_logs = log_target - source_peak - jnp.log(target_sums)
    return (source_logs, target_logs)


def solution(mesh):
    in_specs = (
        P(("blk", "dom"), None),
        P(("blk", "dom"), None),
        P(("blk", "dom"), None),
        P(("blk", "dom"), None),
        P(("blk", "dom"), None),
    )
    out_specs = (P(("blk", "dom"), None), P(("blk", "dom"), None))
    return jax.shard_map(body, mesh=mesh, in_specs=in_specs, out_specs=out_specs, check_vma=False)
```

```python
import math

import jax
import jax.numpy as jnp
from jax import lax
from jax.sharding import PartitionSpec as P

ITERS = 2


entropic = 0.05


def normalized(values):
    widened = values.astype(jnp.float32)
    squared = jnp.sum(widened * widened, axis=1, keepdims=True) + 1e-06
    return (widened * lax.rsqrt(squared)).astype(jnp.bfloat16)


def kernel_block(row_piece, col_piece):
    products = jnp.dot(row_piece, col_piece.T, preferred_element_type=jnp.float32)
    return jnp.exp((products - 1.0) / entropic).astype(jnp.bfloat16)


def segment_sums(row_emb, col_segments, weight_segments, factors, row_block):
    row_count = row_emb.shape[0]
    row_parts = row_emb.reshape(row_count // row_block, row_block, row_emb.shape[1])

    def one_block(row_piece):

        def add_segment(running, paired):
            col_piece, weight_piece, factor = paired
            kernel = kernel_block(row_piece, col_piece)
            part = jnp.dot(kernel, weight_piece, preferred_element_type=jnp.float32)
            return (running + factor[None, :] * part, None)

        initial = jnp.zeros((row_piece.shape[0], weight_segments.shape[-1]), jnp.float32)
        result, unused = lax.scan(add_segment, initial, (col_segments, weight_segments, factors))
        return result

    return lax.map(one_block, row_parts).reshape(row_count, weight_segments.shape[-1])


def plain_sums(row_emb, col_emb, col_weights, row_block, col_block):
    col_count = col_emb.shape[0]
    segments = col_count // col_block
    return segment_sums(
        row_emb,
        col_emb.reshape(segments, col_block, col_emb.shape[1]),
        col_weights.reshape(segments, col_block, col_weights.shape[1]),
        jnp.ones((segments, col_weights.shape[1]), jnp.float32),
        row_block,
    )


def permute_gather(value, axis, count):
    me = lax.axis_index(axis)
    received = [value]
    for shift in range(1, count):
        received.append(lax.ppermute(value, axis, [(i, (i + shift) % count) for i in range(count)]))
    stacked = jnp.stack(received[::-1], 0)
    return jnp.roll(stacked, me + 1, axis=0)


def shift_of(values):
    return jnp.max(values, axis=0).astype(jnp.bfloat16).astype(jnp.float32)


def padded_rows(rows, multiple):
    return -(-rows // multiple) * multiple


def body(source_emb, target_emb, source_counts, target_counts, warm_start):
    blk_count = lax.axis_size("blk")
    dom_count = lax.axis_size("dom")
    src_rows = source_emb.shape[0]
    tgt_rows = target_emb.shape[0]
    columns = warm_start.shape[1]
    width = source_emb.shape[1]
    all_sources = src_rows * blk_count * dom_count
    all_targets = tgt_rows * blk_count * dom_count
    block_rows = src_rows * dom_count
    group_rows = tgt_rows * blk_count

    source_block = lax.all_gather(normalized(source_emb), "dom", axis=0, tiled=True)
    own_targets = normalized(target_emb)
    log_target = jnp.log(target_counts.astype(jnp.float32)) - math.log(all_targets)
    log_source = jnp.log(source_counts.astype(jnp.float32)) - math.log(all_sources)

    tgt_payload_rows = padded_rows(tgt_rows + 1, 16)
    src_piece_rows = padded_rows(src_rows + 1, 8)
    tgt_piece_rows = padded_rows(tgt_rows + 1, 8)

    halves = 2
    half = columns // halves
    target_logs = [warm_start[:, h * half:(h + 1) * half] for h in range(halves)]
    log_targets = [log_target[:, h * half:(h + 1) * half] for h in range(halves)]
    log_sources = [log_source[:, h * half:(h + 1) * half] for h in range(halves)]
    source_logs = [None] * halves
    target_group = None
    kernel = None
    for iteration in range(ITERS):
        for h in range(halves):
            shift = shift_of(target_logs[h])
            weights = jnp.exp(target_logs[h] - shift).astype(jnp.bfloat16)
            payload = jnp.concatenate(
                [weights, shift.astype(jnp.bfloat16)[None, :],
                 jnp.zeros((tgt_payload_rows - tgt_rows - 1, half), jnp.bfloat16)], axis=0)
            if target_group is None:
                emb_rows = jnp.concatenate(
                    [own_targets, jnp.zeros((tgt_payload_rows - tgt_rows, width), jnp.bfloat16)], axis=0)
                payload = jnp.concatenate([emb_rows, payload], axis=1)
                gathered = permute_gather(payload, "blk", blk_count)
                target_group = gathered[:, :tgt_rows, :width].reshape(group_rows, width)
                gathered = gathered[:, :, width:]
            else:
                gathered = permute_gather(payload, "blk", blk_count)
            weight_segments = gathered[:, :tgt_rows, :]
            segment_shift = gathered[:, tgt_rows, :].astype(jnp.float32)
            group_shift = jnp.max(segment_shift, axis=0)
            factors = jnp.exp(segment_shift - group_shift[None, :])
            if kernel is None:
                products = jnp.einsum(
                    "id,sjd->sij", source_block, target_group.reshape(blk_count, tgt_rows, width),
                    preferred_element_type=jnp.float32)
                kernel = jnp.exp((products - 1.0) / entropic).astype(jnp.bfloat16)
            per_segment = jnp.einsum(
                "sij,sjc->sic", kernel, weight_segments, preferred_element_type=jnp.float32)
            partial_value = jnp.sum(per_segment * factors[:, None, :], axis=0)
            pieces = jnp.concatenate(
                [partial_value.reshape(dom_count, src_rows, half),
                 jnp.broadcast_to(group_shift[None, None, :], (dom_count, 1, half)),
                 jnp.zeros((dom_count, src_piece_rows - src_rows - 1, half), jnp.float32)], axis=1)
            received = lax.all_to_all(pieces, "dom", 0, 0, tiled=False)
            group_shifts = received[:, src_rows, :]
            target_peak = jnp.max(group_shifts, axis=0)
            scale = jnp.exp(group_shifts - target_peak[None, :])
            shares = jnp.sum(received[:, :src_rows, :] * scale[:, None, :], axis=0)
            source_logs[h] = log_sources[h] - target_peak - jnp.log(shares)

            block_logs = lax.all_to_all(
                jnp.broadcast_to(source_logs[h][None], (dom_count, src_rows, half)), "dom", 0, 0, tiled=False
            ).reshape(block_rows, half)
            block_peak = jnp.max(block_logs, axis=0)
            source_weights = jnp.exp(block_logs - block_peak).astype(jnp.bfloat16)
            target_partial = jnp.einsum(
                "ic,sij->sjc", source_weights, kernel, preferred_element_type=jnp.float32
            ).reshape(group_rows, half)
            pieces = jnp.concatenate(
                [target_partial.reshape(blk_count, tgt_rows, half),
                 jnp.broadcast_to(block_peak[None, None, :], (blk_count, 1, half)),
                 jnp.zeros((blk_count, tgt_piece_rows - tgt_rows - 1, half), jnp.float32)], axis=1)
            received = lax.all_to_all(pieces, "blk", 0, 0, tiled=False)
            block_peaks = received[:, tgt_rows, :]
            source_peak = jnp.max(block_peaks, axis=0)
            scale = jnp.exp(block_peaks - source_peak[None, :])
            target_sums = jnp.sum(received[:, :tgt_rows, :] * scale[:, None, :], axis=0)
            target_logs[h] = log_targets[h] - source_peak - jnp.log(target_sums)
    source_logs = jnp.concatenate(source_logs, axis=1)
    target_logs = jnp.concatenate(target_logs, axis=1)
    return (source_logs, target_logs)


def solution(mesh):
    in_specs = (
        P(("blk", "dom"), None),
        P(("blk", "dom"), None),
        P(("blk", "dom"), None),
        P(("blk", "dom"), None),
        P(("blk", "dom"), None),
    )
    out_specs = (P(("blk", "dom"), None), P(("blk", "dom"), None))
    return jax.shard_map(body, mesh=mesh, in_specs=in_specs, out_specs=out_specs, check_vma=False)
```

```python
import math

import jax
import jax.numpy as jnp
from jax import lax
from jax.sharding import PartitionSpec as P

ITERS = 2


entropic = 0.05


def normalized(values):
    widened = values.astype(jnp.float32)
    squared = jnp.sum(widened * widened, axis=1, keepdims=True) + 1e-06
    return (widened * lax.rsqrt(squared)).astype(jnp.bfloat16)


def kernel_block(row_piece, col_piece):
    products = jnp.dot(row_piece, col_piece.T, preferred_element_type=jnp.float32)
    return jnp.exp((products - 1.0) / entropic).astype(jnp.bfloat16)


def segment_sums(row_emb, col_segments, weight_segments, factors, row_block):
    row_count = row_emb.shape[0]
    row_parts = row_emb.reshape(row_count // row_block, row_block, row_emb.shape[1])

    def one_block(row_piece):

        def add_segment(running, paired):
            col_piece, weight_piece, factor = paired
            kernel = kernel_block(row_piece, col_piece)
            part = jnp.dot(kernel, weight_piece, preferred_element_type=jnp.float32)
            return (running + factor[None, :] * part, None)

        initial = jnp.zeros((row_piece.shape[0], weight_segments.shape[-1]), jnp.float32)
        result, unused = lax.scan(add_segment, initial, (col_segments, weight_segments, factors))
        return result

    return lax.map(one_block, row_parts).reshape(row_count, weight_segments.shape[-1])


def plain_sums(row_emb, col_emb, col_weights, row_block, col_block):
    col_count = col_emb.shape[0]
    segments = col_count // col_block
    return segment_sums(
        row_emb,
        col_emb.reshape(segments, col_block, col_emb.shape[1]),
        col_weights.reshape(segments, col_block, col_weights.shape[1]),
        jnp.ones((segments, col_weights.shape[1]), jnp.float32),
        row_block,
    )


def permute_gather(value, axis, count):
    me = lax.axis_index(axis)
    received = [value]
    for shift in range(1, count):
        received.append(lax.ppermute(value, axis, [(i, (i + shift) % count) for i in range(count)]))
    stacked = jnp.stack(received[::-1], 0)
    return jnp.roll(stacked, me + 1, axis=0)


def copy_gather(value, axis, count):
    return lax.all_to_all(jnp.broadcast_to(value[None], (count,) + value.shape), axis, 0, 0, tiled=False)


def shift_of(values):
    return jnp.max(values, axis=0).astype(jnp.bfloat16).astype(jnp.float32)


def padded_rows(rows, multiple):
    return -(-rows // multiple) * multiple


def body(source_emb, target_emb, source_counts, target_counts, warm_start):
    blk_count = lax.axis_size("blk")
    dom_count = lax.axis_size("dom")
    src_rows = source_emb.shape[0]
    tgt_rows = target_emb.shape[0]
    columns = warm_start.shape[1]
    width = source_emb.shape[1]
    all_sources = src_rows * blk_count * dom_count
    all_targets = tgt_rows * blk_count * dom_count
    block_rows = src_rows * dom_count
    group_rows = tgt_rows * blk_count

    source_block = copy_gather(normalized(source_emb), "dom", dom_count).reshape(src_rows * dom_count, source_emb.shape[1])
    own_targets = normalized(target_emb)
    log_target = jnp.log(target_counts.astype(jnp.float32)) - math.log(all_targets)
    log_source = jnp.log(source_counts.astype(jnp.float32)) - math.log(all_sources)

    tgt_payload_rows = padded_rows(tgt_rows + 1, 16)
    src_piece_rows = padded_rows(src_rows + 1, 8)
    tgt_piece_rows = padded_rows(tgt_rows + 1, 8)

    target_logs = warm_start
    target_group = None
    source_logs = None
    kernel = None
    for iteration in range(ITERS):
        shift = shift_of(target_logs)
        weights = jnp.exp(target_logs - shift).astype(jnp.bfloat16)
        payload = jnp.concatenate(
            [weights, shift.astype(jnp.bfloat16)[None, :],
             jnp.zeros((tgt_payload_rows - tgt_rows - 1, columns), jnp.bfloat16)], axis=0)
        if target_group is None:
            emb_rows = jnp.concatenate(
                [own_targets, jnp.zeros((tgt_payload_rows - tgt_rows, width), jnp.bfloat16)], axis=0)
            payload = jnp.concatenate([emb_rows, payload], axis=1)
            gathered = copy_gather(payload, "blk", blk_count)
            target_group = gathered[:, :tgt_rows, :width].reshape(group_rows, width)
            gathered = gathered[:, :, width:]
        else:
            gathered = copy_gather(payload, "blk", blk_count)
        weight_segments = gathered[:, :tgt_rows, :]
        segment_shift = gathered[:, tgt_rows, :].astype(jnp.float32)
        group_shift = jnp.max(segment_shift, axis=0)
        factors = jnp.exp(segment_shift - group_shift[None, :])
        if kernel is None:
            products = jnp.einsum(
                "id,sjd->sij", source_block, target_group.reshape(blk_count, tgt_rows, width),
                preferred_element_type=jnp.float32)
            kernel = jnp.exp((products - 1.0) / entropic).astype(jnp.bfloat16)
        per_segment = jnp.einsum(
            "sij,sjc->sic", kernel, weight_segments, preferred_element_type=jnp.float32)
        partial_value = jnp.sum(per_segment * factors[:, None, :], axis=0)
        pieces = jnp.concatenate(
            [partial_value.reshape(dom_count, src_rows, columns),
             jnp.broadcast_to(group_shift[None, None, :], (dom_count, 1, columns)),
             jnp.zeros((dom_count, src_piece_rows - src_rows - 1, columns), jnp.float32)], axis=1)
        received = lax.all_to_all(pieces, "dom", 0, 0, tiled=False)
        group_shifts = received[:, src_rows, :]
        target_peak = jnp.max(group_shifts, axis=0)
        scale = jnp.exp(group_shifts - target_peak[None, :])
        shares = jnp.sum(received[:, :src_rows, :] * scale[:, None, :], axis=0)
        source_logs = log_source - target_peak - jnp.log(shares)

        block_logs = copy_gather(source_logs, "dom", dom_count).reshape(block_rows, columns)
        block_peak = jnp.max(block_logs, axis=0)
        source_weights = jnp.exp(block_logs - block_peak).astype(jnp.bfloat16)
        target_partial = jnp.einsum(
            "ic,sij->sjc", source_weights, kernel, preferred_element_type=jnp.float32
        ).reshape(group_rows, columns)
        pieces = jnp.concatenate(
            [target_partial.reshape(blk_count, tgt_rows, columns),
             jnp.broadcast_to(block_peak[None, None, :], (blk_count, 1, columns)),
             jnp.zeros((blk_count, tgt_piece_rows - tgt_rows - 1, columns), jnp.float32)], axis=1)
        received = lax.all_to_all(pieces, "blk", 0, 0, tiled=False)
        block_peaks = received[:, tgt_rows, :]
        source_peak = jnp.max(block_peaks, axis=0)
        scale = jnp.exp(block_peaks - source_peak[None, :])
        target_sums = jnp.sum(received[:, :tgt_rows, :] * scale[:, None, :], axis=0)
        target_logs = log_target - source_peak - jnp.log(target_sums)
    return (source_logs, target_logs)


def solution(mesh):
    in_specs = (
        P(("blk", "dom"), None),
        P(("blk", "dom"), None),
        P(("blk", "dom"), None),
        P(("blk", "dom"), None),
        P(("blk", "dom"), None),
    )
    out_specs = (P(("blk", "dom"), None), P(("blk", "dom"), None))
    return jax.shard_map(body, mesh=mesh, in_specs=in_specs, out_specs=out_specs, check_vma=False)
```

```python
import math

import jax
import jax.numpy as jnp
from jax import lax
from jax.sharding import PartitionSpec as P

ITERS = 2


entropic = 0.05


def normalized(values):
    widened = values.astype(jnp.float32)
    squared = jnp.sum(widened * widened, axis=1, keepdims=True) + 1e-06
    return (widened * lax.rsqrt(squared)).astype(jnp.bfloat16)


def kernel_block(row_piece, col_piece):
    products = jnp.dot(row_piece, col_piece.T, preferred_element_type=jnp.float32)
    return jnp.exp((products - 1.0) / entropic).astype(jnp.bfloat16)


def segment_sums(row_emb, col_segments, weight_segments, factors, row_block):
    row_count = row_emb.shape[0]
    row_parts = row_emb.reshape(row_count // row_block, row_block, row_emb.shape[1])

    def one_block(row_piece):

        def add_segment(running, paired):
            col_piece, weight_piece, factor = paired
            kernel = kernel_block(row_piece, col_piece)
            part = jnp.dot(kernel, weight_piece, preferred_element_type=jnp.float32)
            return (running + factor[None, :] * part, None)

        initial = jnp.zeros((row_piece.shape[0], weight_segments.shape[-1]), jnp.float32)
        result, unused = lax.scan(add_segment, initial, (col_segments, weight_segments, factors))
        return result

    return lax.map(one_block, row_parts).reshape(row_count, weight_segments.shape[-1])


def plain_sums(row_emb, col_emb, col_weights, row_block, col_block):
    col_count = col_emb.shape[0]
    segments = col_count // col_block
    return segment_sums(
        row_emb,
        col_emb.reshape(segments, col_block, col_emb.shape[1]),
        col_weights.reshape(segments, col_block, col_weights.shape[1]),
        jnp.ones((segments, col_weights.shape[1]), jnp.float32),
        row_block,
    )


def permute_gather(value, axis, count):
    me = lax.axis_index(axis)
    received = [value]
    for shift in range(1, count):
        received.append(lax.ppermute(value, axis, [(i, (i + shift) % count) for i in range(count)]))
    stacked = jnp.stack(received[::-1], 0)
    return jnp.roll(stacked, me + 1, axis=0)


def copy_gather(value, axis, count):
    return lax.all_to_all(jnp.broadcast_to(value[None], (count,) + value.shape), axis, 0, 0, tiled=False)


def shift_of(values):
    return jnp.max(values, axis=0).astype(jnp.bfloat16).astype(jnp.float32)


def padded_rows(rows, multiple):
    return -(-rows // multiple) * multiple


def body(source_emb, target_emb, source_counts, target_counts, warm_start):
    blk_count = lax.axis_size("blk")
    dom_count = lax.axis_size("dom")
    src_rows = source_emb.shape[0]
    tgt_rows = target_emb.shape[0]
    columns = warm_start.shape[1]
    width = source_emb.shape[1]
    all_sources = src_rows * blk_count * dom_count
    all_targets = tgt_rows * blk_count * dom_count
    block_rows = src_rows * dom_count
    group_rows = tgt_rows * blk_count

    source_block = permute_gather(normalized(source_emb), "dom", dom_count).reshape(
        src_rows * dom_count, source_emb.shape[1])
    own_targets = normalized(target_emb)
    log_target = jnp.log(target_counts.astype(jnp.float32)) - math.log(all_targets)
    log_source = jnp.log(source_counts.astype(jnp.float32)) - math.log(all_sources)

    tgt_payload_rows = padded_rows(tgt_rows + 1, 16)
    src_piece_rows = padded_rows(src_rows + 1, 8)
    src_payload_rows = padded_rows(src_rows + 1, 16)
    tgt_piece_rows = padded_rows(tgt_rows + 1, 8)

    target_logs = warm_start
    target_group = None
    source_logs = None
    kernel = None
    for iteration in range(ITERS):
        shift = shift_of(target_logs)
        weights = jnp.exp(target_logs - shift).astype(jnp.bfloat16)
        payload = jnp.concatenate(
            [weights, shift.astype(jnp.bfloat16)[None, :],
             jnp.zeros((tgt_payload_rows - tgt_rows - 1, columns), jnp.bfloat16)], axis=0)
        if target_group is None:
            emb_rows = jnp.concatenate(
                [own_targets, jnp.zeros((tgt_payload_rows - tgt_rows, width), jnp.bfloat16)], axis=0)
            payload = jnp.concatenate([emb_rows, payload], axis=1)
            gathered = copy_gather(payload, "blk", blk_count)
            target_group = gathered[:, :tgt_rows, :width].reshape(group_rows, width)
            gathered = gathered[:, :, width:]
        else:
            gathered = copy_gather(payload, "blk", blk_count)
        weight_segments = gathered[:, :tgt_rows, :]
        segment_shift = gathered[:, tgt_rows, :].astype(jnp.float32)
        group_shift = jnp.max(segment_shift, axis=0)
        factors = jnp.exp(segment_shift - group_shift[None, :])
        if kernel is None:
            products = jnp.einsum(
                "id,sjd->sij", source_block, target_group.reshape(blk_count, tgt_rows, width),
                preferred_element_type=jnp.float32)
            kernel = jnp.exp((products - 1.0) / entropic).astype(jnp.bfloat16)
        per_segment = jnp.einsum(
            "sij,sjc->sic", kernel, weight_segments, preferred_element_type=jnp.float32)
        partial_value = jnp.sum(per_segment * factors[:, None, :], axis=0)
        pieces = jnp.concatenate(
            [partial_value.reshape(dom_count, src_rows, columns),
             jnp.broadcast_to(group_shift[None, None, :], (dom_count, 1, columns)),
             jnp.zeros((dom_count, src_piece_rows - src_rows - 1, columns), jnp.float32)], axis=1)
        received = lax.all_to_all(pieces, "dom", 0, 0, tiled=False)
        group_shifts = received[:, src_rows, :]
        target_peak = jnp.max(group_shifts, axis=0)
        scale = jnp.exp(group_shifts - target_peak[None, :])
        shares = jnp.sum(received[:, :src_rows, :] * scale[:, None, :], axis=0)
        source_logs = log_source - target_peak - jnp.log(shares)

        own_shift = shift_of(source_logs)
        own_weights = jnp.exp(source_logs - own_shift).astype(jnp.bfloat16)
        payload = jnp.concatenate(
            [own_weights, own_shift.astype(jnp.bfloat16)[None, :],
             jnp.zeros((src_payload_rows - src_rows - 1, columns), jnp.bfloat16)], axis=0)
        gathered = copy_gather(payload, "dom", dom_count)
        owner_shift = gathered[:, src_rows, :].astype(jnp.float32)
        block_peak = jnp.max(owner_shift, axis=0)
        owner_factor = jnp.exp(owner_shift - block_peak[None, :])
        source_weights = (gathered[:, :src_rows, :].astype(jnp.float32) * owner_factor[:, None, :]).astype(
            jnp.bfloat16).reshape(block_rows, columns)
        target_partial = jnp.einsum(
            "ic,sij->sjc", source_weights, kernel, preferred_element_type=jnp.float32
        ).reshape(group_rows, columns)
        pieces = jnp.concatenate(
            [target_partial.reshape(blk_count, tgt_rows, columns),
             jnp.broadcast_to(block_peak[None, None, :], (blk_count, 1, columns)),
             jnp.zeros((blk_count, tgt_piece_rows - tgt_rows - 1, columns), jnp.float32)], axis=1)
        received = lax.all_to_all(pieces, "blk", 0, 0, tiled=False)
        block_peaks = received[:, tgt_rows, :]
        source_peak = jnp.max(block_peaks, axis=0)
        scale = jnp.exp(block_peaks - source_peak[None, :])
        target_sums = jnp.sum(received[:, :tgt_rows, :] * scale[:, None, :], axis=0)
        target_logs = log_target - source_peak - jnp.log(target_sums)
    return (source_logs, target_logs)


def solution(mesh):
    in_specs = (
        P(("blk", "dom"), None),
        P(("blk", "dom"), None),
        P(("blk", "dom"), None),
        P(("blk", "dom"), None),
        P(("blk", "dom"), None),
    )
    out_specs = (P(("blk", "dom"), None), P(("blk", "dom"), None))
    return jax.shard_map(body, mesh=mesh, in_specs=in_specs, out_specs=out_specs, check_vma=False)
```

```python
import math

import jax
import jax.numpy as jnp
from jax import lax
from jax.sharding import PartitionSpec as P

ITERS = 2


entropic = 0.05


def normalized(values):
    widened = values.astype(jnp.float32)
    squared = jnp.sum(widened * widened, axis=1, keepdims=True) + 1e-06
    return (widened * lax.rsqrt(squared)).astype(jnp.bfloat16)


def kernel_block(row_piece, col_piece):
    products = jnp.dot(row_piece, col_piece.T, preferred_element_type=jnp.float32)
    return jnp.exp((products - 1.0) / entropic).astype(jnp.bfloat16)


def segment_sums(row_emb, col_segments, weight_segments, factors, row_block):
    row_count = row_emb.shape[0]
    row_parts = row_emb.reshape(row_count // row_block, row_block, row_emb.shape[1])

    def one_block(row_piece):

        def add_segment(running, paired):
            col_piece, weight_piece, factor = paired
            kernel = kernel_block(row_piece, col_piece)
            part = jnp.dot(kernel, weight_piece, preferred_element_type=jnp.float32)
            return (running + factor[None, :] * part, None)

        initial = jnp.zeros((row_piece.shape[0], weight_segments.shape[-1]), jnp.float32)
        result, unused = lax.scan(add_segment, initial, (col_segments, weight_segments, factors))
        return result

    return lax.map(one_block, row_parts).reshape(row_count, weight_segments.shape[-1])


def plain_sums(row_emb, col_emb, col_weights, row_block, col_block):
    col_count = col_emb.shape[0]
    segments = col_count // col_block
    return segment_sums(
        row_emb,
        col_emb.reshape(segments, col_block, col_emb.shape[1]),
        col_weights.reshape(segments, col_block, col_weights.shape[1]),
        jnp.ones((segments, col_weights.shape[1]), jnp.float32),
        row_block,
    )


def permute_gather(value, axis, count):
    me = lax.axis_index(axis)
    received = [value]
    for shift in range(1, count):
        received.append(lax.ppermute(value, axis, [(i, (i + shift) % count) for i in range(count)]))
    stacked = jnp.stack(received[::-1], 0)
    return jnp.roll(stacked, me + 1, axis=0)


def copy_gather(value, axis, count):
    return lax.all_to_all(jnp.broadcast_to(value[None], (count,) + value.shape), axis, 0, 0, tiled=False)


def shift_of(values):
    return jnp.max(values, axis=0).astype(jnp.bfloat16).astype(jnp.float32)


def padded_rows(rows, multiple):
    return -(-rows // multiple) * multiple


def body(source_emb, target_emb, source_counts, target_counts, warm_start):
    blk_count = lax.axis_size("blk")
    dom_count = lax.axis_size("dom")
    src_rows = source_emb.shape[0]
    tgt_rows = target_emb.shape[0]
    columns = warm_start.shape[1]
    width = source_emb.shape[1]
    all_sources = src_rows * blk_count * dom_count
    all_targets = tgt_rows * blk_count * dom_count
    block_rows = src_rows * dom_count
    group_rows = tgt_rows * blk_count

    source_block = copy_gather(normalized(source_emb), "dom", dom_count).reshape(
        src_rows * dom_count, source_emb.shape[1])
    target_group = copy_gather(normalized(target_emb), "blk", blk_count).reshape(
        tgt_rows * blk_count, target_emb.shape[1])
    products = jnp.einsum(
        "id,sjd->sij", source_block, target_group.reshape(blk_count, tgt_rows, source_emb.shape[1]),
        preferred_element_type=jnp.float32)
    kernel = jnp.exp((products - 1.0) / entropic).astype(jnp.bfloat16)
    log_target = jnp.log(target_counts.astype(jnp.float32)) - math.log(all_targets)
    log_source = jnp.log(source_counts.astype(jnp.float32)) - math.log(all_sources)

    tgt_payload_rows = padded_rows(tgt_rows + 1, 16)
    src_piece_rows = padded_rows(src_rows + 1, 8)
    src_payload_rows = padded_rows(src_rows + 1, 16)
    tgt_piece_rows = padded_rows(tgt_rows + 1, 8)

    target_logs = warm_start
    source_logs = None
    for iteration in range(ITERS):
        shift = shift_of(target_logs)
        weights = jnp.exp(target_logs - shift).astype(jnp.bfloat16)
        payload = jnp.concatenate(
            [weights, shift.astype(jnp.bfloat16)[None, :],
             jnp.zeros((tgt_payload_rows - tgt_rows - 1, columns), jnp.bfloat16)], axis=0)
        gathered = copy_gather(payload, "blk", blk_count)
        weight_segments = gathered[:, :tgt_rows, :]
        segment_shift = gathered[:, tgt_rows, :].astype(jnp.float32)
        group_shift = jnp.max(segment_shift, axis=0)
        factors = jnp.exp(segment_shift - group_shift[None, :])
        per_segment = jnp.einsum(
            "sij,sjc->sic", kernel, weight_segments, preferred_element_type=jnp.float32)
        partial_value = jnp.sum(per_segment * factors[:, None, :], axis=0)
        pieces = jnp.concatenate(
            [partial_value.reshape(dom_count, src_rows, columns),
             jnp.broadcast_to(group_shift[None, None, :], (dom_count, 1, columns)),
             jnp.zeros((dom_count, src_piece_rows - src_rows - 1, columns), jnp.float32)], axis=1)
        received = lax.all_to_all(pieces, "dom", 0, 0, tiled=False)
        group_shifts = received[:, src_rows, :]
        target_peak = jnp.max(group_shifts, axis=0)
        scale = jnp.exp(group_shifts - target_peak[None, :])
        shares = jnp.sum(received[:, :src_rows, :] * scale[:, None, :], axis=0)
        source_logs = log_source - target_peak - jnp.log(shares)

        own_shift = shift_of(source_logs)
        own_weights = jnp.exp(source_logs - own_shift).astype(jnp.bfloat16)
        payload = jnp.concatenate(
            [own_weights, own_shift.astype(jnp.bfloat16)[None, :],
             jnp.zeros((src_payload_rows - src_rows - 1, columns), jnp.bfloat16)], axis=0)
        gathered = copy_gather(payload, "dom", dom_count)
        owner_shift = gathered[:, src_rows, :].astype(jnp.float32)
        block_peak = jnp.max(owner_shift, axis=0)
        owner_factor = jnp.exp(owner_shift - block_peak[None, :])
        source_weights = (gathered[:, :src_rows, :].astype(jnp.float32) * owner_factor[:, None, :]).astype(
            jnp.bfloat16).reshape(block_rows, columns)
        target_partial = jnp.einsum(
            "ic,sij->sjc", source_weights, kernel, preferred_element_type=jnp.float32
        ).reshape(group_rows, columns)
        pieces = jnp.concatenate(
            [target_partial.reshape(blk_count, tgt_rows, columns),
             jnp.broadcast_to(block_peak[None, None, :], (blk_count, 1, columns)),
             jnp.zeros((blk_count, tgt_piece_rows - tgt_rows - 1, columns), jnp.float32)], axis=1)
        received = lax.all_to_all(pieces, "blk", 0, 0, tiled=False)
        block_peaks = received[:, tgt_rows, :]
        source_peak = jnp.max(block_peaks, axis=0)
        scale = jnp.exp(block_peaks - source_peak[None, :])
        target_sums = jnp.sum(received[:, :tgt_rows, :] * scale[:, None, :], axis=0)
        target_logs = log_target - source_peak - jnp.log(target_sums)
    return (source_logs, target_logs)


def solution(mesh):
    in_specs = (
        P(("blk", "dom"), None),
        P(("blk", "dom"), None),
        P(("blk", "dom"), None),
        P(("blk", "dom"), None),
        P(("blk", "dom"), None),
    )
    out_specs = (P(("blk", "dom"), None), P(("blk", "dom"), None))
    return jax.shard_map(body, mesh=mesh, in_specs=in_specs, out_specs=out_specs, check_vma=False)
```

```python
import math

import jax
import jax.numpy as jnp
from jax import lax
from jax.sharding import PartitionSpec as P

ITERS = 2


entropic = 0.05


def normalized(values):
    widened = values.astype(jnp.float32)
    squared = jnp.sum(widened * widened, axis=1, keepdims=True) + 1e-06
    return (widened * lax.rsqrt(squared)).astype(jnp.bfloat16)


def kernel_block(row_piece, col_piece):
    products = jnp.dot(row_piece, col_piece.T, preferred_element_type=jnp.float32)
    return jnp.exp((products - 1.0) / entropic).astype(jnp.bfloat16)


def segment_sums(row_emb, col_segments, weight_segments, factors, row_block):
    row_count = row_emb.shape[0]
    row_parts = row_emb.reshape(row_count // row_block, row_block, row_emb.shape[1])

    def one_block(row_piece):

        def add_segment(running, paired):
            col_piece, weight_piece, factor = paired
            kernel = kernel_block(row_piece, col_piece)
            part = jnp.dot(kernel, weight_piece, preferred_element_type=jnp.float32)
            return (running + factor[None, :] * part, None)

        initial = jnp.zeros((row_piece.shape[0], weight_segments.shape[-1]), jnp.float32)
        result, unused = lax.scan(add_segment, initial, (col_segments, weight_segments, factors))
        return result

    return lax.map(one_block, row_parts).reshape(row_count, weight_segments.shape[-1])


def plain_sums(row_emb, col_emb, col_weights, row_block, col_block):
    col_count = col_emb.shape[0]
    segments = col_count // col_block
    return segment_sums(
        row_emb,
        col_emb.reshape(segments, col_block, col_emb.shape[1]),
        col_weights.reshape(segments, col_block, col_weights.shape[1]),
        jnp.ones((segments, col_weights.shape[1]), jnp.float32),
        row_block,
    )


def permute_gather(value, axis, count):
    me = lax.axis_index(axis)
    received = [value]
    for shift in range(1, count):
        received.append(lax.ppermute(value, axis, [(i, (i + shift) % count) for i in range(count)]))
    stacked = jnp.stack(received[::-1], 0)
    return jnp.roll(stacked, me + 1, axis=0)


def copy_gather(value, axis, count):
    return lax.all_to_all(jnp.broadcast_to(value[None], (count,) + value.shape), axis, 0, 0, tiled=False)


def shift_of(values):
    return jnp.max(values, axis=0).astype(jnp.bfloat16).astype(jnp.float32)


def padded_rows(rows, multiple):
    return -(-rows // multiple) * multiple


def body(source_emb, target_emb, source_counts, target_counts, warm_start):
    blk_count = lax.axis_size("blk")
    dom_count = lax.axis_size("dom")
    src_rows = source_emb.shape[0]
    tgt_rows = target_emb.shape[0]
    columns = warm_start.shape[1]
    width = source_emb.shape[1]
    all_sources = src_rows * blk_count * dom_count
    all_targets = tgt_rows * blk_count * dom_count
    block_rows = src_rows * dom_count
    group_rows = tgt_rows * blk_count

    source_block = copy_gather(normalized(source_emb), "dom", dom_count).reshape(
        src_rows * dom_count, source_emb.shape[1])
    target_group = permute_gather(normalized(target_emb), "blk", blk_count).reshape(
        tgt_rows * blk_count, target_emb.shape[1])
    products = jnp.einsum(
        "id,sjd->sij", source_block, target_group.reshape(blk_count, tgt_rows, source_emb.shape[1]),
        preferred_element_type=jnp.float32)
    kernel = jnp.exp((products - 1.0) / entropic).astype(jnp.bfloat16)
    log_target = jnp.log(target_counts.astype(jnp.float32)) - math.log(all_targets)
    log_source = jnp.log(source_counts.astype(jnp.float32)) - math.log(all_sources)

    tgt_payload_rows = padded_rows(tgt_rows + 1, 16)
    src_piece_rows = padded_rows(src_rows + 1, 8)
    src_payload_rows = padded_rows(src_rows + 1, 16)
    tgt_piece_rows = padded_rows(tgt_rows + 1, 8)

    target_logs = warm_start
    source_logs = None
    for iteration in range(ITERS):
        shift = shift_of(target_logs)
        weights = jnp.exp(target_logs - shift).astype(jnp.bfloat16)
        payload = jnp.concatenate(
            [weights, shift.astype(jnp.bfloat16)[None, :],
             jnp.zeros((tgt_payload_rows - tgt_rows - 1, columns), jnp.bfloat16)], axis=0)
        gathered = copy_gather(payload, "blk", blk_count)
        weight_segments = gathered[:, :tgt_rows, :]
        segment_shift = gathered[:, tgt_rows, :].astype(jnp.float32)
        group_shift = jnp.max(segment_shift, axis=0)
        factors = jnp.exp(segment_shift - group_shift[None, :])
        per_segment = jnp.einsum(
            "sij,sjc->sic", kernel, weight_segments, preferred_element_type=jnp.float32)
        partial_value = jnp.sum(per_segment * factors[:, None, :], axis=0)
        pieces = jnp.concatenate(
            [partial_value.reshape(dom_count, src_rows, columns),
             jnp.broadcast_to(group_shift[None, None, :], (dom_count, 1, columns)),
             jnp.zeros((dom_count, src_piece_rows - src_rows - 1, columns), jnp.float32)], axis=1)
        received = lax.all_to_all(pieces, "dom", 0, 0, tiled=False)
        group_shifts = received[:, src_rows, :]
        target_peak = jnp.max(group_shifts, axis=0)
        scale = jnp.exp(group_shifts - target_peak[None, :])
        shares = jnp.sum(received[:, :src_rows, :] * scale[:, None, :], axis=0)
        source_logs = log_source - target_peak - jnp.log(shares)

        own_shift = shift_of(source_logs)
        own_weights = jnp.exp(source_logs - own_shift).astype(jnp.bfloat16)
        payload = jnp.concatenate(
            [own_weights, own_shift.astype(jnp.bfloat16)[None, :],
             jnp.zeros((src_payload_rows - src_rows - 1, columns), jnp.bfloat16)], axis=0)
        gathered = copy_gather(payload, "dom", dom_count)
        owner_shift = gathered[:, src_rows, :].astype(jnp.float32)
        block_peak = jnp.max(owner_shift, axis=0)
        owner_factor = jnp.exp(owner_shift - block_peak[None, :])
        source_weights = (gathered[:, :src_rows, :].astype(jnp.float32) * owner_factor[:, None, :]).astype(
            jnp.bfloat16).reshape(block_rows, columns)
        target_partial = jnp.einsum(
            "ic,sij->sjc", source_weights, kernel, preferred_element_type=jnp.float32
        ).reshape(group_rows, columns)
        pieces = jnp.concatenate(
            [target_partial.reshape(blk_count, tgt_rows, columns),
             jnp.broadcast_to(block_peak[None, None, :], (blk_count, 1, columns)),
             jnp.zeros((blk_count, tgt_piece_rows - tgt_rows - 1, columns), jnp.float32)], axis=1)
        received = lax.all_to_all(pieces, "blk", 0, 0, tiled=False)
        block_peaks = received[:, tgt_rows, :]
        source_peak = jnp.max(block_peaks, axis=0)
        scale = jnp.exp(block_peaks - source_peak[None, :])
        target_sums = jnp.sum(received[:, :tgt_rows, :] * scale[:, None, :], axis=0)
        target_logs = log_target - source_peak - jnp.log(target_sums)
    return (source_logs, target_logs)


def solution(mesh):
    in_specs = (
        P(("blk", "dom"), None),
        P(("blk", "dom"), None),
        P(("blk", "dom"), None),
        P(("blk", "dom"), None),
        P(("blk", "dom"), None),
    )
    out_specs = (P(("blk", "dom"), None), P(("blk", "dom"), None))
    return jax.shard_map(body, mesh=mesh, in_specs=in_specs, out_specs=out_specs, check_vma=False)
```

```python
import math

import jax
import jax.numpy as jnp
from jax import lax
from jax.sharding import PartitionSpec as P

ITERS = 2


entropic = 0.05


def normalized(values):
    widened = values.astype(jnp.float32)
    squared = jnp.sum(widened * widened, axis=1, keepdims=True) + 1e-06
    return (widened * lax.rsqrt(squared)).astype(jnp.bfloat16)


def kernel_block(row_piece, col_piece):
    products = jnp.dot(row_piece, col_piece.T, preferred_element_type=jnp.float32)
    return jnp.exp((products - 1.0) / entropic).astype(jnp.bfloat16)


def segment_sums(row_emb, col_segments, weight_segments, factors, row_block):
    row_count = row_emb.shape[0]
    row_parts = row_emb.reshape(row_count // row_block, row_block, row_emb.shape[1])

    def one_block(row_piece):

        def add_segment(running, paired):
            col_piece, weight_piece, factor = paired
            kernel = kernel_block(row_piece, col_piece)
            part = jnp.dot(kernel, weight_piece, preferred_element_type=jnp.float32)
            return (running + factor[None, :] * part, None)

        initial = jnp.zeros((row_piece.shape[0], weight_segments.shape[-1]), jnp.float32)
        result, unused = lax.scan(add_segment, initial, (col_segments, weight_segments, factors))
        return result

    return lax.map(one_block, row_parts).reshape(row_count, weight_segments.shape[-1])


def plain_sums(row_emb, col_emb, col_weights, row_block, col_block):
    col_count = col_emb.shape[0]
    segments = col_count // col_block
    return segment_sums(
        row_emb,
        col_emb.reshape(segments, col_block, col_emb.shape[1]),
        col_weights.reshape(segments, col_block, col_weights.shape[1]),
        jnp.ones((segments, col_weights.shape[1]), jnp.float32),
        row_block,
    )


def permute_gather(value, axis, count):
    me = lax.axis_index(axis)
    received = [value]
    for shift in range(1, count):
        received.append(lax.ppermute(value, axis, [(i, (i + shift) % count) for i in range(count)]))
    stacked = jnp.stack(received[::-1], 0)
    return jnp.roll(stacked, me + 1, axis=0)


def copy_gather(value, axis, count):
    return lax.all_to_all(jnp.broadcast_to(value[None], (count,) + value.shape), axis, 0, 0, tiled=False)


def shift_of(values):
    return jnp.max(values, axis=0).astype(jnp.bfloat16).astype(jnp.float32)


def padded_rows(rows, multiple):
    return -(-rows // multiple) * multiple


def body(source_emb, target_emb, source_counts, target_counts, warm_start):
    blk_count = lax.axis_size("blk")
    dom_count = lax.axis_size("dom")
    src_rows = source_emb.shape[0]
    tgt_rows = target_emb.shape[0]
    columns = warm_start.shape[1]
    width = source_emb.shape[1]
    all_sources = src_rows * blk_count * dom_count
    all_targets = tgt_rows * blk_count * dom_count
    block_rows = src_rows * dom_count
    group_rows = tgt_rows * blk_count

    source_block = copy_gather(normalized(source_emb), "dom", dom_count).reshape(
        src_rows * dom_count, source_emb.shape[1])
    target_group = copy_gather(normalized(target_emb), "blk", blk_count).reshape(
        tgt_rows * blk_count, target_emb.shape[1])
    products = jnp.einsum(
        "id,sjd->sij", source_block, target_group.reshape(blk_count, tgt_rows, source_emb.shape[1]),
        preferred_element_type=jnp.float32)
    kernel = jnp.exp((products - 1.0) / entropic).astype(jnp.bfloat16)
    log_target = jnp.log(target_counts.astype(jnp.float32)) - math.log(all_targets)
    log_source = jnp.log(source_counts.astype(jnp.float32)) - math.log(all_sources)

    tgt_payload_rows = padded_rows(tgt_rows + 1, 16)
    src_piece_rows = padded_rows(src_rows + 1, 8)
    src_payload_rows = padded_rows(src_rows + 1, 16)
    tgt_piece_rows = padded_rows(tgt_rows + 1, 8)

    target_logs = warm_start
    source_logs = None
    for iteration in range(ITERS):
        shift = shift_of(target_logs)
        weights = jnp.exp(target_logs - shift).astype(jnp.bfloat16)
        payload = jnp.concatenate(
            [weights, shift.astype(jnp.bfloat16)[None, :],
             jnp.zeros((tgt_payload_rows - tgt_rows - 1, columns), jnp.bfloat16)], axis=0)
        if iteration == 0:
            gathered = lax.all_gather(payload, "blk", axis=0, tiled=False)
        else:
            gathered = copy_gather(payload, "blk", blk_count)
        weight_segments = gathered[:, :tgt_rows, :]
        segment_shift = gathered[:, tgt_rows, :].astype(jnp.float32)
        group_shift = jnp.max(segment_shift, axis=0)
        factors = jnp.exp(segment_shift - group_shift[None, :])
        per_segment = jnp.einsum(
            "sij,sjc->sic", kernel, weight_segments, preferred_element_type=jnp.float32)
        partial_value = jnp.sum(per_segment * factors[:, None, :], axis=0)
        pieces = jnp.concatenate(
            [partial_value.reshape(dom_count, src_rows, columns),
             jnp.broadcast_to(group_shift[None, None, :], (dom_count, 1, columns)),
             jnp.zeros((dom_count, src_piece_rows - src_rows - 1, columns), jnp.float32)], axis=1)
        received = lax.all_to_all(pieces, "dom", 0, 0, tiled=False)
        group_shifts = received[:, src_rows, :]
        target_peak = jnp.max(group_shifts, axis=0)
        scale = jnp.exp(group_shifts - target_peak[None, :])
        shares = jnp.sum(received[:, :src_rows, :] * scale[:, None, :], axis=0)
        source_logs = log_source - target_peak - jnp.log(shares)

        own_shift = shift_of(source_logs)
        own_weights = jnp.exp(source_logs - own_shift).astype(jnp.bfloat16)
        payload = jnp.concatenate(
            [own_weights, own_shift.astype(jnp.bfloat16)[None, :],
             jnp.zeros((src_payload_rows - src_rows - 1, columns), jnp.bfloat16)], axis=0)
        gathered = copy_gather(payload, "dom", dom_count)
        owner_shift = gathered[:, src_rows, :].astype(jnp.float32)
        block_peak = jnp.max(owner_shift, axis=0)
        owner_factor = jnp.exp(owner_shift - block_peak[None, :])
        source_weights = (gathered[:, :src_rows, :].astype(jnp.float32) * owner_factor[:, None, :]).astype(
            jnp.bfloat16).reshape(block_rows, columns)
        target_partial = jnp.einsum(
            "ic,sij->sjc", source_weights, kernel, preferred_element_type=jnp.float32
        ).reshape(group_rows, columns)
        pieces = jnp.concatenate(
            [target_partial.reshape(blk_count, tgt_rows, columns),
             jnp.broadcast_to(block_peak[None, None, :], (blk_count, 1, columns)),
             jnp.zeros((blk_count, tgt_piece_rows - tgt_rows - 1, columns), jnp.float32)], axis=1)
        received = lax.all_to_all(pieces, "blk", 0, 0, tiled=False)
        block_peaks = received[:, tgt_rows, :]
        source_peak = jnp.max(block_peaks, axis=0)
        scale = jnp.exp(block_peaks - source_peak[None, :])
        target_sums = jnp.sum(received[:, :tgt_rows, :] * scale[:, None, :], axis=0)
        target_logs = log_target - source_peak - jnp.log(target_sums)
    return (source_logs, target_logs)


def solution(mesh):
    in_specs = (
        P(("blk", "dom"), None),
        P(("blk", "dom"), None),
        P(("blk", "dom"), None),
        P(("blk", "dom"), None),
        P(("blk", "dom"), None),
    )
    out_specs = (P(("blk", "dom"), None), P(("blk", "dom"), None))
    return jax.shard_map(body, mesh=mesh, in_specs=in_specs, out_specs=out_specs, check_vma=False)
```

```python
import math

import jax
import jax.numpy as jnp
from jax import lax
from jax.sharding import PartitionSpec as P

ITERS = 2


entropic = 0.05


def normalized(values):
    widened = values.astype(jnp.float32)
    squared = jnp.sum(widened * widened, axis=1, keepdims=True) + 1e-06
    return (widened * lax.rsqrt(squared)).astype(jnp.bfloat16)


def kernel_block(row_piece, col_piece):
    products = jnp.dot(row_piece, col_piece.T, preferred_element_type=jnp.float32)
    return jnp.exp((products - 1.0) / entropic).astype(jnp.bfloat16)


def segment_sums(row_emb, col_segments, weight_segments, factors, row_block):
    row_count = row_emb.shape[0]
    row_parts = row_emb.reshape(row_count // row_block, row_block, row_emb.shape[1])

    def one_block(row_piece):

        def add_segment(running, paired):
            col_piece, weight_piece, factor = paired
            kernel = kernel_block(row_piece, col_piece)
            part = jnp.dot(kernel, weight_piece, preferred_element_type=jnp.float32)
            return (running + factor[None, :] * part, None)

        initial = jnp.zeros((row_piece.shape[0], weight_segments.shape[-1]), jnp.float32)
        result, unused = lax.scan(add_segment, initial, (col_segments, weight_segments, factors))
        return result

    return lax.map(one_block, row_parts).reshape(row_count, weight_segments.shape[-1])


def plain_sums(row_emb, col_emb, col_weights, row_block, col_block):
    col_count = col_emb.shape[0]
    segments = col_count // col_block
    return segment_sums(
        row_emb,
        col_emb.reshape(segments, col_block, col_emb.shape[1]),
        col_weights.reshape(segments, col_block, col_weights.shape[1]),
        jnp.ones((segments, col_weights.shape[1]), jnp.float32),
        row_block,
    )


def permute_gather(value, axis, count):
    me = lax.axis_index(axis)
    received = [value]
    for shift in range(1, count):
        received.append(lax.ppermute(value, axis, [(i, (i + shift) % count) for i in range(count)]))
    stacked = jnp.stack(received[::-1], 0)
    return jnp.roll(stacked, me + 1, axis=0)


def copy_gather(value, axis, count):
    return lax.all_to_all(jnp.broadcast_to(value[None], (count,) + value.shape), axis, 0, 0, tiled=False)


def shift_of(values):
    return jnp.max(values, axis=0).astype(jnp.bfloat16).astype(jnp.float32)


def padded_rows(rows, multiple):
    return -(-rows // multiple) * multiple


def body(source_emb, target_emb, source_counts, target_counts, warm_start):
    blk_count = lax.axis_size("blk")
    dom_count = lax.axis_size("dom")
    src_rows = source_emb.shape[0]
    tgt_rows = target_emb.shape[0]
    columns = warm_start.shape[1]
    width = source_emb.shape[1]
    all_sources = src_rows * blk_count * dom_count
    all_targets = tgt_rows * blk_count * dom_count
    block_rows = src_rows * dom_count
    group_rows = tgt_rows * blk_count

    source_block = copy_gather(normalized(source_emb), "dom", dom_count).reshape(
        src_rows * dom_count, source_emb.shape[1])
    target_group = copy_gather(normalized(target_emb), "blk", blk_count).reshape(
        tgt_rows * blk_count, target_emb.shape[1])
    products = jnp.einsum(
        "id,sjd->sij", source_block, target_group.reshape(blk_count, tgt_rows, source_emb.shape[1]),
        preferred_element_type=jnp.float32)
    kernel = jnp.exp((products - 1.0) / entropic).astype(jnp.bfloat16)
    log_target = jnp.log(target_counts.astype(jnp.float32)) - math.log(all_targets)
    log_source = jnp.log(source_counts.astype(jnp.float32)) - math.log(all_sources)

    tgt_payload_rows = padded_rows(tgt_rows + 1, 16)
    src_piece_rows = padded_rows(src_rows + 1, 8)
    src_payload_rows = padded_rows(src_rows + 1, 16)
    tgt_piece_rows = padded_rows(tgt_rows + 1, 8)

    target_logs = warm_start
    source_logs = None
    for iteration in range(ITERS):
        shift = shift_of(target_logs)
        weights = jnp.exp(target_logs - shift).astype(jnp.bfloat16)
        payload = jnp.concatenate(
            [weights, shift.astype(jnp.bfloat16)[None, :],
             jnp.zeros((tgt_payload_rows - tgt_rows - 1, columns), jnp.bfloat16)], axis=0)
        gathered = copy_gather(payload, "blk", blk_count)
        weight_segments = gathered[:, :tgt_rows, :]
        segment_shift = gathered[:, tgt_rows, :].astype(jnp.float32)
        group_shift = jnp.max(segment_shift, axis=0)
        factors = jnp.exp(segment_shift - group_shift[None, :])
        per_segment = jnp.einsum(
            "sij,sjc->sic", kernel, weight_segments, preferred_element_type=jnp.float32)
        partial_value = jnp.sum(per_segment * factors[:, None, :], axis=0)
        pieces = jnp.concatenate(
            [partial_value.reshape(dom_count, src_rows, columns),
             jnp.broadcast_to(group_shift[None, None, :], (dom_count, 1, columns)),
             jnp.zeros((dom_count, src_payload_rows - src_rows - 1, columns), jnp.float32)], axis=1)
        received = lax.all_to_all(pieces.astype(jnp.bfloat16), "dom", 0, 0, tiled=False).astype(jnp.float32)
        group_shifts = received[:, src_rows, :]
        target_peak = jnp.max(group_shifts, axis=0)
        scale = jnp.exp(group_shifts - target_peak[None, :])
        shares = jnp.sum(received[:, :src_rows, :] * scale[:, None, :], axis=0)
        source_logs = log_source - target_peak - jnp.log(shares)

        own_shift = shift_of(source_logs)
        own_weights = jnp.exp(source_logs - own_shift).astype(jnp.bfloat16)
        payload = jnp.concatenate(
            [own_weights, own_shift.astype(jnp.bfloat16)[None, :],
             jnp.zeros((src_payload_rows - src_rows - 1, columns), jnp.bfloat16)], axis=0)
        gathered = copy_gather(payload, "dom", dom_count)
        owner_shift = gathered[:, src_rows, :].astype(jnp.float32)
        block_peak = jnp.max(owner_shift, axis=0)
        owner_factor = jnp.exp(owner_shift - block_peak[None, :])
        source_weights = (gathered[:, :src_rows, :].astype(jnp.float32) * owner_factor[:, None, :]).astype(
            jnp.bfloat16).reshape(block_rows, columns)
        target_partial = jnp.einsum(
            "ic,sij->sjc", source_weights, kernel, preferred_element_type=jnp.float32
        ).reshape(group_rows, columns)
        pieces = jnp.concatenate(
            [target_partial.reshape(blk_count, tgt_rows, columns),
             jnp.broadcast_to(block_peak[None, None, :], (blk_count, 1, columns)),
             jnp.zeros((blk_count, tgt_payload_rows - tgt_rows - 1, columns), jnp.float32)], axis=1)
        received = lax.all_to_all(pieces.astype(jnp.bfloat16), "blk", 0, 0, tiled=False).astype(jnp.float32)
        block_peaks = received[:, tgt_rows, :]
        source_peak = jnp.max(block_peaks, axis=0)
        scale = jnp.exp(block_peaks - source_peak[None, :])
        target_sums = jnp.sum(received[:, :tgt_rows, :] * scale[:, None, :], axis=0)
        target_logs = log_target - source_peak - jnp.log(target_sums)
    return (source_logs, target_logs)


def solution(mesh):
    in_specs = (
        P(("blk", "dom"), None),
        P(("blk", "dom"), None),
        P(("blk", "dom"), None),
        P(("blk", "dom"), None),
        P(("blk", "dom"), None),
    )
    out_specs = (P(("blk", "dom"), None), P(("blk", "dom"), None))
    return jax.shard_map(body, mesh=mesh, in_specs=in_specs, out_specs=out_specs, check_vma=False)
```

```python
import math

import jax
import jax.numpy as jnp
from jax import lax
from jax.sharding import PartitionSpec as P

ITERS = 2


entropic = 0.05


def normalized(values):
    widened = values.astype(jnp.float32)
    squared = jnp.sum(widened * widened, axis=1, keepdims=True) + 1e-06
    return (widened * lax.rsqrt(squared)).astype(jnp.bfloat16)


def kernel_block(row_piece, col_piece):
    products = jnp.dot(row_piece, col_piece.T, preferred_element_type=jnp.float32)
    return jnp.exp((products - 1.0) / entropic).astype(jnp.bfloat16)


def segment_sums(row_emb, col_segments, weight_segments, factors, row_block):
    row_count = row_emb.shape[0]
    row_parts = row_emb.reshape(row_count // row_block, row_block, row_emb.shape[1])

    def one_block(row_piece):

        def add_segment(running, paired):
            col_piece, weight_piece, factor = paired
            kernel = kernel_block(row_piece, col_piece)
            part = jnp.dot(kernel, weight_piece, preferred_element_type=jnp.float32)
            return (running + factor[None, :] * part, None)

        initial = jnp.zeros((row_piece.shape[0], weight_segments.shape[-1]), jnp.float32)
        result, unused = lax.scan(add_segment, initial, (col_segments, weight_segments, factors))
        return result

    return lax.map(one_block, row_parts).reshape(row_count, weight_segments.shape[-1])


def plain_sums(row_emb, col_emb, col_weights, row_block, col_block):
    col_count = col_emb.shape[0]
    segments = col_count // col_block
    return segment_sums(
        row_emb,
        col_emb.reshape(segments, col_block, col_emb.shape[1]),
        col_weights.reshape(segments, col_block, col_weights.shape[1]),
        jnp.ones((segments, col_weights.shape[1]), jnp.float32),
        row_block,
    )


def permute_gather(value, axis, count):
    me = lax.axis_index(axis)
    received = [value]
    for shift in range(1, count):
        received.append(lax.ppermute(value, axis, [(i, (i + shift) % count) for i in range(count)]))
    stacked = jnp.stack(received[::-1], 0)
    return jnp.roll(stacked, me + 1, axis=0)


def copy_gather(value, axis, count):
    return lax.all_to_all(jnp.broadcast_to(value[None], (count,) + value.shape), axis, 0, 0, tiled=False)


def shift_of(values):
    return jnp.max(values, axis=0).astype(jnp.bfloat16).astype(jnp.float32)


def padded_rows(rows, multiple):
    return -(-rows // multiple) * multiple


def body(source_emb, target_emb, source_counts, target_counts, warm_start):
    blk_count = lax.axis_size("blk")
    dom_count = lax.axis_size("dom")
    src_rows = source_emb.shape[0]
    tgt_rows = target_emb.shape[0]
    columns = warm_start.shape[1]
    width = source_emb.shape[1]
    all_sources = src_rows * blk_count * dom_count
    all_targets = tgt_rows * blk_count * dom_count
    block_rows = src_rows * dom_count
    group_rows = tgt_rows * blk_count

    source_block = copy_gather(normalized(source_emb), "dom", dom_count).reshape(
        src_rows * dom_count, source_emb.shape[1])
    target_group = copy_gather(normalized(target_emb), "blk", blk_count).reshape(
        tgt_rows * blk_count, target_emb.shape[1])
    products = jnp.einsum(
        "id,sjd->sij", source_block, target_group.reshape(blk_count, tgt_rows, source_emb.shape[1]),
        preferred_element_type=jnp.float32)
    kernel = jnp.exp((products - 1.0) / entropic).astype(jnp.bfloat16)
    log_target = jnp.log(target_counts.astype(jnp.float32)) - math.log(all_targets)
    log_source = jnp.log(source_counts.astype(jnp.float32)) - math.log(all_sources)

    tgt_payload_rows = padded_rows(tgt_rows + 1, 16)
    src_piece_rows = padded_rows(src_rows + 1, 8)
    src_payload_rows = padded_rows(src_rows + 1, 16)
    tgt_piece_rows = padded_rows(tgt_rows + 1, 8)

    target_logs = warm_start
    source_logs = None
    for iteration in range(ITERS):
        shift = shift_of(target_logs)
        weights = jnp.exp(target_logs - shift).astype(jnp.bfloat16)
        payload = jnp.concatenate(
            [weights, shift.astype(jnp.bfloat16)[None, :],
             jnp.zeros((tgt_payload_rows - tgt_rows - 1, columns), jnp.bfloat16)], axis=0)
        gathered = copy_gather(payload, "blk", blk_count)
        weight_segments = gathered[:, :tgt_rows, :]
        segment_shift = gathered[:, tgt_rows, :].astype(jnp.float32)
        group_shift = jnp.max(segment_shift, axis=0)
        factors = jnp.exp(segment_shift - group_shift[None, :])
        scaled_segments = (weight_segments.astype(jnp.float32) * factors[:, None, :]).astype(jnp.bfloat16)
        partial_value = jnp.einsum(
            "sij,sjc->ic", kernel, scaled_segments, preferred_element_type=jnp.float32)
        pieces = jnp.concatenate(
            [partial_value.reshape(dom_count, src_rows, columns),
             jnp.broadcast_to(group_shift[None, None, :], (dom_count, 1, columns)),
             jnp.zeros((dom_count, src_payload_rows - src_rows - 1, columns), jnp.float32)], axis=1)
        received = lax.all_to_all(pieces.astype(jnp.bfloat16), "dom", 0, 0, tiled=False).astype(jnp.float32)
        group_shifts = received[:, src_rows, :]
        target_peak = jnp.max(group_shifts, axis=0)
        scale = jnp.exp(group_shifts - target_peak[None, :])
        shares = jnp.sum(received[:, :src_rows, :] * scale[:, None, :], axis=0)
        source_logs = log_source - target_peak - jnp.log(shares)

        own_shift = shift_of(source_logs)
        own_weights = jnp.exp(source_logs - own_shift).astype(jnp.bfloat16)
        payload = jnp.concatenate(
            [own_weights, own_shift.astype(jnp.bfloat16)[None, :],
             jnp.zeros((src_payload_rows - src_rows - 1, columns), jnp.bfloat16)], axis=0)
        gathered = copy_gather(payload, "dom", dom_count)
        owner_shift = gathered[:, src_rows, :].astype(jnp.float32)
        block_peak = jnp.max(owner_shift, axis=0)
        owner_factor = jnp.exp(owner_shift - block_peak[None, :])
        source_weights = (gathered[:, :src_rows, :].astype(jnp.float32) * owner_factor[:, None, :]).astype(
            jnp.bfloat16).reshape(block_rows, columns)
        target_partial = jnp.einsum(
            "ic,sij->sjc", source_weights, kernel, preferred_element_type=jnp.float32
        ).reshape(group_rows, columns)
        pieces = jnp.concatenate(
            [target_partial.reshape(blk_count, tgt_rows, columns),
             jnp.broadcast_to(block_peak[None, None, :], (blk_count, 1, columns)),
             jnp.zeros((blk_count, tgt_payload_rows - tgt_rows - 1, columns), jnp.float32)], axis=1)
        received = lax.all_to_all(pieces.astype(jnp.bfloat16), "blk", 0, 0, tiled=False).astype(jnp.float32)
        block_peaks = received[:, tgt_rows, :]
        source_peak = jnp.max(block_peaks, axis=0)
        scale = jnp.exp(block_peaks - source_peak[None, :])
        target_sums = jnp.sum(received[:, :tgt_rows, :] * scale[:, None, :], axis=0)
        target_logs = log_target - source_peak - jnp.log(target_sums)
    return (source_logs, target_logs)


def solution(mesh):
    in_specs = (
        P(("blk", "dom"), None),
        P(("blk", "dom"), None),
        P(("blk", "dom"), None),
        P(("blk", "dom"), None),
        P(("blk", "dom"), None),
    )
    out_specs = (P(("blk", "dom"), None), P(("blk", "dom"), None))
    return jax.shard_map(body, mesh=mesh, in_specs=in_specs, out_specs=out_specs, check_vma=False)
```

```python
import math

import jax
import jax.numpy as jnp
from jax import lax
from jax.sharding import PartitionSpec as P

ITERS = 2


entropic = 0.05


def normalized(values):
    widened = values.astype(jnp.float32)
    squared = jnp.sum(widened * widened, axis=1, keepdims=True) + 1e-06
    return (widened * lax.rsqrt(squared)).astype(jnp.bfloat16)


def copy_gather(value, axis, count):
    return lax.all_to_all(jnp.broadcast_to(value[None], (count,) + value.shape), axis, 0, 0, tiled=False)


def shift_of(values):
    return jnp.max(values, axis=0).astype(jnp.bfloat16).astype(jnp.float32)


def padded_rows(rows, multiple):
    return -(-rows // multiple) * multiple


def body(source_emb, target_emb, source_counts, target_counts, warm_start):
    blk_count = lax.axis_size("blk")
    dom_count = lax.axis_size("dom")
    src_rows = source_emb.shape[0]
    tgt_rows = target_emb.shape[0]
    columns = warm_start.shape[1]
    all_sources = src_rows * blk_count * dom_count
    all_targets = tgt_rows * blk_count * dom_count
    block_rows = src_rows * dom_count
    group_rows = tgt_rows * blk_count

    source_block = copy_gather(normalized(source_emb), "dom", dom_count).reshape(
        src_rows * dom_count, source_emb.shape[1])
    target_group = copy_gather(normalized(target_emb), "blk", blk_count).reshape(
        tgt_rows * blk_count, target_emb.shape[1])
    products = jnp.einsum(
        "id,sjd->sij", source_block, target_group.reshape(blk_count, tgt_rows, source_emb.shape[1]),
        preferred_element_type=jnp.float32)
    kernel = jnp.exp((products - 1.0) / entropic).astype(jnp.bfloat16)
    log_target = jnp.log(target_counts.astype(jnp.float32)) - math.log(all_targets)
    log_source = jnp.log(source_counts.astype(jnp.float32)) - math.log(all_sources)

    tgt_payload_rows = padded_rows(tgt_rows + 1, 16)
    src_payload_rows = padded_rows(src_rows + 1, 16)

    target_logs = warm_start
    source_logs = None
    for iteration in range(ITERS):
        shift = shift_of(target_logs)
        weights = jnp.exp(target_logs - shift).astype(jnp.bfloat16)
        payload = jnp.concatenate(
            [weights, shift.astype(jnp.bfloat16)[None, :],
             jnp.zeros((tgt_payload_rows - tgt_rows - 1, columns), jnp.bfloat16)], axis=0)
        gathered = copy_gather(payload, "blk", blk_count)
        weight_segments = gathered[:, :tgt_rows, :]
        segment_shift = gathered[:, tgt_rows, :].astype(jnp.float32)
        group_shift = jnp.max(segment_shift, axis=0)
        factors = jnp.exp(segment_shift - group_shift[None, :])
        scaled_segments = (weight_segments.astype(jnp.float32) * factors[:, None, :]).astype(jnp.bfloat16)
        partial_value = jnp.einsum(
            "sij,sjc->ic", kernel, scaled_segments, preferred_element_type=jnp.float32)
        pieces = jnp.concatenate(
            [partial_value.reshape(dom_count, src_rows, columns),
             jnp.broadcast_to(group_shift[None, None, :], (dom_count, 1, columns)),
             jnp.zeros((dom_count, src_payload_rows - src_rows - 1, columns), jnp.float32)], axis=1)
        received = lax.all_to_all(pieces.astype(jnp.bfloat16), "dom", 0, 0, tiled=False).astype(jnp.float32)
        group_shifts = received[:, src_rows, :]
        target_peak = jnp.max(group_shifts, axis=0)
        scale = jnp.exp(group_shifts - target_peak[None, :])
        shares = jnp.sum(received[:, :src_rows, :] * scale[:, None, :], axis=0)
        source_logs = log_source - target_peak - jnp.log(shares)

        own_shift = shift_of(source_logs)
        own_weights = jnp.exp(source_logs - own_shift).astype(jnp.bfloat16)
        payload = jnp.concatenate(
            [own_weights, own_shift.astype(jnp.bfloat16)[None, :],
             jnp.zeros((src_payload_rows - src_rows - 1, columns), jnp.bfloat16)], axis=0)
        gathered = copy_gather(payload, "dom", dom_count)
        owner_shift = gathered[:, src_rows, :].astype(jnp.float32)
        block_peak = jnp.max(owner_shift, axis=0)
        owner_factor = jnp.exp(owner_shift - block_peak[None, :])
        source_weights = (gathered[:, :src_rows, :].astype(jnp.float32) * owner_factor[:, None, :]).astype(
            jnp.bfloat16).reshape(block_rows, columns)
        target_partial = jnp.einsum(
            "ic,sij->sjc", source_weights, kernel, preferred_element_type=jnp.float32
        ).reshape(group_rows, columns)
        pieces = jnp.concatenate(
            [target_partial.reshape(blk_count, tgt_rows, columns),
             jnp.broadcast_to(block_peak[None, None, :], (blk_count, 1, columns)),
             jnp.zeros((blk_count, tgt_payload_rows - tgt_rows - 1, columns), jnp.float32)], axis=1)
        received = lax.all_to_all(pieces.astype(jnp.bfloat16), "blk", 0, 0, tiled=False).astype(jnp.float32)
        block_peaks = received[:, tgt_rows, :]
        source_peak = jnp.max(block_peaks, axis=0)
        scale = jnp.exp(block_peaks - source_peak[None, :])
        target_sums = jnp.sum(received[:, :tgt_rows, :] * scale[:, None, :], axis=0)
        target_logs = log_target - source_peak - jnp.log(target_sums)
    return (source_logs, target_logs)


def solution(mesh):
    in_specs = (
        P(("blk", "dom"), None),
        P(("blk", "dom"), None),
        P(("blk", "dom"), None),
        P(("blk", "dom"), None),
        P(("blk", "dom"), None),
    )
    out_specs = (P(("blk", "dom"), None), P(("blk", "dom"), None))
    return jax.shard_map(body, mesh=mesh, in_specs=in_specs, out_specs=out_specs, check_vma=False)
```

```python
import math

import jax
import jax.numpy as jnp
from jax import lax
from jax.sharding import PartitionSpec as P


ITERS = 2


entropic = 0.05


def normalized(values):
    widened = values.astype(jnp.float32)
    squared = jnp.sum(widened * widened, axis=1, keepdims=True) + 1e-06
    return (widened * lax.rsqrt(squared)).astype(jnp.bfloat16)


def copy_gather(value, axis, count):
    return lax.all_to_all(jnp.broadcast_to(value[None], (count,) + value.shape), axis, 0, 0, tiled=False)


def shift_of(values):
    return jnp.max(values, axis=0).astype(jnp.bfloat16).astype(jnp.float32)


def padded_rows(rows, multiple):
    return -(-rows // multiple) * multiple


def steps(source_emb, target_emb, source_counts, target_counts, warm_start):
    blk_count = lax.axis_size("blk")
    dom_count = lax.axis_size("dom")
    src_rows = source_emb.shape[0]
    tgt_rows = target_emb.shape[0]
    columns = warm_start.shape[1]
    all_sources = src_rows * blk_count * dom_count
    all_targets = tgt_rows * blk_count * dom_count
    block_rows = src_rows * dom_count
    group_rows = tgt_rows * blk_count

    source_block = copy_gather(normalized(source_emb), "dom", dom_count).reshape(
        src_rows * dom_count, source_emb.shape[1])
    target_copies = jnp.broadcast_to(normalized(target_emb)[None], (blk_count,) + target_emb.shape)
    target_group = lax.all_to_all(target_copies, "blk", 0, 0, tiled=False).reshape(
        tgt_rows * blk_count, target_emb.shape[1])
    products = jnp.einsum(
        "id,sjd->sij", source_block, target_group.reshape(blk_count, tgt_rows, source_emb.shape[1]),
        preferred_element_type=jnp.float32)
    kernel = jnp.exp((products - 1.0) / entropic).astype(jnp.bfloat16)
    log_target = jnp.log(target_counts.astype(jnp.float32)) - math.log(all_targets)
    log_source = jnp.log(source_counts.astype(jnp.float32)) - math.log(all_sources)

    tgt_payload_rows = padded_rows(tgt_rows + 1, 16)
    src_payload_rows = padded_rows(src_rows + 1, 16)

    target_logs = warm_start
    source_logs = None
    for iteration in range(ITERS):
        shift = shift_of(target_logs)
        weights = jnp.exp(target_logs - shift).astype(jnp.bfloat16)
        payload = jnp.concatenate(
            [weights, shift.astype(jnp.bfloat16)[None, :],
             jnp.zeros((tgt_payload_rows - tgt_rows - 1, columns), jnp.bfloat16)], axis=0)
        if iteration == 0:
            copies = jnp.broadcast_to(payload[None], (blk_count,) + payload.shape)
            gathered = lax.all_to_all(copies, "blk", 0, 0, tiled=False)
        else:
            gathered = copy_gather(payload, "blk", blk_count)
        weight_segments = gathered[:, :tgt_rows, :]
        segment_shift = gathered[:, tgt_rows, :].astype(jnp.float32)
        group_shift = jnp.max(segment_shift, axis=0)
        factors = jnp.exp(segment_shift - group_shift[None, :])
        scaled_segments = (weight_segments.astype(jnp.float32) * factors[:, None, :]).astype(jnp.bfloat16)
        partial_value = jnp.einsum(
            "sij,sjc->ic", kernel, scaled_segments, preferred_element_type=jnp.float32)
        pieces = jnp.concatenate(
            [partial_value.reshape(dom_count, src_rows, columns),
             jnp.broadcast_to(group_shift[None, None, :], (dom_count, 1, columns)),
             jnp.zeros((dom_count, src_payload_rows - src_rows - 1, columns), jnp.float32)], axis=1)
        received = lax.all_to_all(pieces.astype(jnp.bfloat16), "dom", 0, 0, tiled=False).astype(jnp.float32)
        group_shifts = received[:, src_rows, :]
        target_peak = jnp.max(group_shifts, axis=0)
        scale = jnp.exp(group_shifts - target_peak[None, :])
        shares = jnp.sum(received[:, :src_rows, :] * scale[:, None, :], axis=0)
        source_logs = log_source - target_peak - jnp.log(shares)

        own_shift = shift_of(source_logs)
        own_weights = jnp.exp(source_logs - own_shift).astype(jnp.bfloat16)
        payload = jnp.concatenate(
            [own_weights, own_shift.astype(jnp.bfloat16)[None, :],
             jnp.zeros((src_payload_rows - src_rows - 1, columns), jnp.bfloat16)], axis=0)
        gathered = copy_gather(payload, "dom", dom_count)
        owner_shift = gathered[:, src_rows, :].astype(jnp.float32)
        block_peak = jnp.max(owner_shift, axis=0)
        owner_factor = jnp.exp(owner_shift - block_peak[None, :])
        source_weights = (gathered[:, :src_rows, :].astype(jnp.float32) * owner_factor[:, None, :]).astype(
            jnp.bfloat16).reshape(block_rows, columns)
        target_partial = jnp.einsum(
            "ic,sij->sjc", source_weights, kernel, preferred_element_type=jnp.float32
        ).reshape(group_rows, columns)
        pieces = jnp.concatenate(
            [target_partial.reshape(blk_count, tgt_rows, columns),
             jnp.broadcast_to(block_peak[None, None, :], (blk_count, 1, columns)),
             jnp.zeros((blk_count, tgt_payload_rows - tgt_rows - 1, columns), jnp.float32)], axis=1)
        received = lax.all_to_all(pieces.astype(jnp.bfloat16), "blk", 0, 0, tiled=False).astype(jnp.float32)
        block_peaks = received[:, tgt_rows, :]
        source_peak = jnp.max(block_peaks, axis=0)
        scale = jnp.exp(block_peaks - source_peak[None, :])
        target_sums = jnp.sum(received[:, :tgt_rows, :] * scale[:, None, :], axis=0)
        target_logs = log_target - source_peak - jnp.log(target_sums)
    return (source_logs, target_logs)


def solution(mesh):
    in_specs = (
        P(("blk", "dom"), None),
        P(("blk", "dom"), None),
        P(("blk", "dom"), None),
        P(("blk", "dom"), None),
        P(("blk", "dom"), None),
    )
    out_specs = (P(("blk", "dom"), None), P(("blk", "dom"), None))
    return jax.shard_map(steps, mesh=mesh, in_specs=in_specs, out_specs=out_specs, check_vma=False)
```

```python
import math

import jax
import jax.numpy as jnp
from jax import lax
from jax.sharding import PartitionSpec as P


ITERS = 2


entropic = 0.05


def normalized(values):
    widened = values.astype(jnp.float32)
    squared = jnp.sum(widened * widened, axis=1, keepdims=True) + 1e-06
    return (widened * lax.rsqrt(squared)).astype(jnp.bfloat16)


def copy_gather(value, axis, count):
    return lax.all_to_all(jnp.broadcast_to(value[None], (count,) + value.shape), axis, 0, 0, tiled=False)


def shift_of(values):
    return jnp.max(values, axis=0).astype(jnp.bfloat16).astype(jnp.float32)


def padded_rows(rows, multiple):
    return -(-rows // multiple) * multiple


def steps(source_emb, target_emb, source_counts, target_counts, warm_start):
    blk_count = lax.axis_size("blk")
    dom_count = lax.axis_size("dom")
    src_rows = source_emb.shape[0]
    tgt_rows = target_emb.shape[0]
    columns = warm_start.shape[1]
    all_sources = src_rows * blk_count * dom_count
    all_targets = tgt_rows * blk_count * dom_count
    block_rows = src_rows * dom_count
    group_rows = tgt_rows * blk_count

    raw_block = copy_gather(source_emb, "dom", dom_count).reshape(src_rows * dom_count, source_emb.shape[1])
    target_copies = jnp.broadcast_to(normalized(target_emb)[None], (blk_count,) + target_emb.shape)
    target_group = lax.all_to_all(target_copies, "blk", 0, 0, tiled=False).reshape(
        tgt_rows * blk_count, target_emb.shape[1])
    source_block = normalized(raw_block)
    products = jnp.einsum(
        "id,sjd->sij", source_block, target_group.reshape(blk_count, tgt_rows, source_emb.shape[1]),
        preferred_element_type=jnp.float32)
    kernel = jnp.exp((products - 1.0) / entropic).astype(jnp.bfloat16)
    log_target, log_source = lax.optimization_barrier((
        jnp.log(target_counts.astype(jnp.float32)) - math.log(all_targets),
        jnp.log(source_counts.astype(jnp.float32)) - math.log(all_sources)))

    tgt_payload_rows = padded_rows(tgt_rows + 1, 16)
    src_payload_rows = padded_rows(src_rows + 1, 16)

    target_logs = warm_start
    source_logs = None
    for iteration in range(ITERS):
        shift = shift_of(target_logs)
        weights = jnp.exp(target_logs - shift).astype(jnp.bfloat16)
        payload = jnp.concatenate(
            [weights, shift.astype(jnp.bfloat16)[None, :],
             jnp.zeros((tgt_payload_rows - tgt_rows - 1, columns), jnp.bfloat16)], axis=0)
        if iteration == 0:
            copies = jnp.broadcast_to(payload[None], (blk_count,) + payload.shape)
            gathered = lax.all_to_all(copies, "blk", 0, 0, tiled=False)
        else:
            gathered = copy_gather(payload, "blk", blk_count)
        weight_segments = gathered[:, :tgt_rows, :]
        segment_shift = gathered[:, tgt_rows, :].astype(jnp.float32)
        group_shift = jnp.max(segment_shift, axis=0)
        factors = jnp.exp(segment_shift - group_shift[None, :])
        scaled_segments = (weight_segments.astype(jnp.float32) * factors[:, None, :]).astype(jnp.bfloat16)
        partial_value = jnp.einsum(
            "sij,sjc->ic", kernel, scaled_segments, preferred_element_type=jnp.float32)
        pieces = jnp.concatenate(
            [partial_value.reshape(dom_count, src_rows, columns),
             jnp.broadcast_to(group_shift[None, None, :], (dom_count, 1, columns)),
             jnp.zeros((dom_count, src_payload_rows - src_rows - 1, columns), jnp.float32)], axis=1)
        received = lax.all_to_all(pieces.astype(jnp.bfloat16), "dom", 0, 0, tiled=False).astype(jnp.float32)
        group_shifts = received[:, src_rows, :]
        target_peak = jnp.max(group_shifts, axis=0)
        scale = jnp.exp(group_shifts - target_peak[None, :])
        shares = jnp.sum(received[:, :src_rows, :] * scale[:, None, :], axis=0)
        source_logs = log_source - target_peak - jnp.log(shares)

        own_shift = shift_of(source_logs)
        own_weights = jnp.exp(source_logs - own_shift).astype(jnp.bfloat16)
        payload = jnp.concatenate(
            [own_weights, own_shift.astype(jnp.bfloat16)[None, :],
             jnp.zeros((src_payload_rows - src_rows - 1, columns), jnp.bfloat16)], axis=0)
        gathered = copy_gather(payload, "dom", dom_count)
        owner_shift = gathered[:, src_rows, :].astype(jnp.float32)
        block_peak = jnp.max(owner_shift, axis=0)
        owner_factor = jnp.exp(owner_shift - block_peak[None, :])
        source_weights = (gathered[:, :src_rows, :].astype(jnp.float32) * owner_factor[:, None, :]).astype(
            jnp.bfloat16).reshape(block_rows, columns)
        target_partial = jnp.einsum(
            "ic,sij->sjc", source_weights, kernel, preferred_element_type=jnp.float32
        ).reshape(group_rows, columns)
        pieces = jnp.concatenate(
            [target_partial.reshape(blk_count, tgt_rows, columns),
             jnp.broadcast_to(block_peak[None, None, :], (blk_count, 1, columns)),
             jnp.zeros((blk_count, tgt_payload_rows - tgt_rows - 1, columns), jnp.float32)], axis=1)
        received = lax.all_to_all(pieces.astype(jnp.bfloat16), "blk", 0, 0, tiled=False).astype(jnp.float32)
        block_peaks = received[:, tgt_rows, :]
        source_peak = jnp.max(block_peaks, axis=0)
        scale = jnp.exp(block_peaks - source_peak[None, :])
        target_sums = jnp.sum(received[:, :tgt_rows, :] * scale[:, None, :], axis=0)
        target_logs = log_target - source_peak - jnp.log(target_sums)
    return (source_logs, target_logs)


def solution(mesh):
    in_specs = (
        P(("blk", "dom"), None),
        P(("blk", "dom"), None),
        P(("blk", "dom"), None),
        P(("blk", "dom"), None),
        P(("blk", "dom"), None),
    )
    out_specs = (P(("blk", "dom"), None), P(("blk", "dom"), None))
    return jax.shard_map(steps, mesh=mesh, in_specs=in_specs, out_specs=out_specs, check_vma=False)
```
